256 devices in a mesh: samp: 64 (over x, z, core), blk: 4 (over y).
Axes of the slice: x: 4, y: 4, z: 8, core: 2. Of those that a mesh axis runs over, the one named last changes fastest.
Arguments:
- dosages: bfloat16 [40960, 2048], P('samp', 'blk'), may hold values from 0 to 2
- traits: bfloat16 [16, 40960], P(None, 'samp'), may hold values from -6 to 6
- folds: int32 [40960], P('samp'), may hold values from 0 to 4
Outputs:
- level0: float32 [4, 5, 16, 40960], P(None, None, 'blk', 'samp')
- blend: float32 [16, 40960], P('blk', 'samp')
The draws below stay inside these ranges and needn't reach their ends.
All inputs are finite; a program needn't handle non-finite values.
Results may differ from the reference program's by a relative error of at most 0.0097.
Values may be sent and summed in bfloat16 or wider, within the bound.
No kernel may reach another device: no remote copies, remote signals or barrier semaphores. Data moves between devices by JAX's collectives and lax.ppermute only.
A program may use at most 64 MiB of HBM per device.

```python
import math
import jax
import jax.numpy as jnp
from jax import lax

VB = 512
TRAITS = 16
FOLDS = 5
SHRINK = 5
BLOCKS = 4
VARIANTS = 2048
SAMPLES = 40960


def draw_dosages(key, part):
    key_freq, key_rows, key_own, key_shared, key_weight = jax.random.split(key, 5)
    frequency = jnp.exp(jax.random.uniform(key_freq, (1, VARIANTS), jnp.float32, math.log(0.05), math.log(0.5)))
    position = jnp.arange(SAMPLES, dtype=jnp.float32)[:, None] / SAMPLES
    run_count = (VARIANTS + 31) // 32
    run_weight = jax.random.uniform(key_weight, (1, run_count), jnp.float32, 0.5, 0.85)
    run_weight = jnp.repeat(run_weight, 32, axis=1)[:, :VARIANTS]
    row_scale = jnp.exp(math.log(3.0) * position) * jnp.exp(jax.random.uniform(key_rows, (SAMPLES, 1), jnp.float32, 0.0, math.log(3.5)))
    own_noise = jax.random.exponential(key_own, (SAMPLES, VARIANTS), jnp.float32)
    shared_noise = jax.random.exponential(key_shared, (SAMPLES, run_count), jnp.float32)
    shared_noise = jnp.repeat(shared_noise, 32, axis=1)[:, :VARIANTS]
    mixture = (1.0 - run_weight) * own_noise + run_weight * shared_noise
    dosage_value = 2.0 * (1.0 - jnp.exp(-frequency * row_scale * mixture))
    return dosage_value.astype(jnp.bfloat16)


def place_ends(entries, stream_key, smallest, high):
    spot = [jax.random.randint(jax.random.fold_in(stream_key, axis), (), 0, length) for axis, length in enumerate(entries.shape)]
    main_axis = entries.shape.index(max(entries.shape))
    neighbour = spot[:main_axis] + [(spot[main_axis] + 1) % entries.shape[main_axis]] + spot[main_axis + 1:]
    return entries.at[tuple(spot)].set(smallest).at[tuple(neighbour)].set(high)


def levels(stream_key, shape, cuts, low, top_value):
    def one(axis_at, shards_of):
        heights = jax.random.uniform(jax.random.fold_in(jax.random.fold_in(stream_key, 6), axis_at), (shards_of,), jnp.float32, low / len(cuts), top_value / len(cuts))
        return jnp.repeat(jnp.exp(heights), shape[axis_at] // shards_of).reshape((-1,) + (1,) * (len(shape) - axis_at - 1))

    level = one(*cuts[0])
    for cut in cuts[1:]:
        level = level * one(*cut)
    return level


def gaussian(own_key, shape, scale, bound, cuts=(), kind=jnp.bfloat16):
    values = scale * jax.random.normal(own_key, shape, jnp.float32)
    if cuts:
        values = values * levels(own_key, shape, cuts, -0.22, 0.18)
    return jnp.clip(values, -bound, bound).astype(kind)


def setup_inputs(seed: int = 0) -> dict:
    key_list = jax.random.split(jax.random.key(seed), 4)
    return {
        "dosages": draw_dosages(jax.random.fold_in(key_list[3], 71), 0),
        "traits": gaussian(key_list[1], (TRAITS, SAMPLES), 1.0, 6.0, ((1, 64),)),
        "folds": place_ends(jax.random.randint(key_list[2], (SAMPLES,), 0, FOLDS), jax.random.fold_in(key_list[2], 1), 0, FOLDS - 1).astype(jnp.int32),
    }


RATIOS = (99.0, 3.0, 1.0, 1.0 / 3.0, 1.0 / 99.0)
EPS = 1e-05
HIGH = lax.Precision.HIGHEST

def solve_batch(systems, right_sides):
    factors = jnp.linalg.cholesky(systems)

    def solve_single(factor, right_side):
        return jax.scipy.linalg.cho_solve((factor, True), right_side)
    return jax.vmap(solve_single)(factors, right_sides)

def reference(dosages, traits, folds):
    fold_ids = jnp.arange(FOLDS, dtype=jnp.int32)
    masks = (folds[None, :] == fold_ids[:, None]).astype(jnp.float32)
    mask_half = masks.astype(jnp.bfloat16)
    traits_wide = traits.astype(jnp.float32)
    trait_sums = jnp.einsum('ks,ts->kt', masks, traits_wide, precision=HIGH)
    counts = lax.optimization_barrier(jnp.sum(masks, axis=1))
    ratios = jnp.array(RATIOS, dtype=jnp.float32)
    identity = jnp.eye(VB, dtype=jnp.float32)
    total = jnp.sum(counts)
    block_preds = []
    for block in range(BLOCKS):
        columns = dosages[:, block * VB:(block + 1) * VB]
        grams = []
        crosses = []
        for fold in range(FOLDS):
            weighted = columns * mask_half[fold][:, None]
            grams.append(jnp.dot(columns.T.astype(jnp.float32), weighted.astype(jnp.float32), preferred_element_type=jnp.float32))
            crosses.append(jnp.dot((traits * mask_half[fold][None, :]).astype(jnp.float32), columns.astype(jnp.float32), preferred_element_type=jnp.float32))
        gram = jnp.stack(grams)
        cross = jnp.stack(crosses)
        sums = jnp.dot(mask_half.astype(jnp.float32), columns.astype(jnp.float32), preferred_element_type=jnp.float32)
        mean = lax.optimization_barrier(jnp.sum(sums, axis=0)) / SAMPLES
        gram_total = lax.optimization_barrier(jnp.sum(gram, axis=0))
        variance = jnp.diagonal(gram_total) / SAMPLES - mean * mean
        scale = lax.rsqrt(variance + EPS)
        sums_total = lax.optimization_barrier(jnp.sum(sums, axis=0))
        cross_total = lax.optimization_barrier(jnp.sum(cross, axis=0))
        trait_total = lax.optimization_barrier(jnp.sum(trait_sums, axis=0))
        accum = jnp.zeros((SHRINK, TRAITS, SAMPLES), jnp.float32)
        for fold in range(FOLDS):
            train_gram = gram_total - gram[fold]
            train_sums = sums_total - sums[fold]
            train_count = total - counts[fold]
            train_cross = cross_total - cross[fold]
            train_traits = trait_total - trait_sums[fold]
            centered = train_gram - mean[:, None] * train_sums[None, :] - train_sums[:, None] * mean[None, :] + train_count * mean[:, None] * mean[None, :]
            system = scale[:, None] * centered * scale[None, :]
            target = scale[:, None] * (train_cross.T - mean[:, None] * train_traits[None, :])
            shrunk = system[None] + (ratios * VB)[:, None, None] * identity[None]
            beta = solve_batch(shrunk, jnp.broadcast_to(target, (SHRINK,) + target.shape))
            coef = (scale[None, :, None] * beta).astype(jnp.bfloat16)
            shift = jnp.einsum('v,lvt->lt', mean, coef.astype(jnp.float32), precision=HIGH)
            for shrink in range(SHRINK):
                pred = jnp.dot(columns.astype(jnp.float32), coef[shrink].astype(jnp.float32), preferred_element_type=jnp.float32) - shift[shrink][None, :]
                accum = accum.at[shrink].add(pred.T * masks[fold][None, :])
        block_preds.append(accum)
    preds = jnp.stack(block_preds)
    pmean = lax.optimization_barrier(jnp.sum(preds, axis=-1)) / SAMPLES
    pvar = lax.optimization_barrier(jnp.sum(preds * preds, axis=-1)) / SAMPLES - pmean * pmean
    level0 = (preds - pmean[..., None]) * lax.rsqrt(pvar + EPS)[..., None]
    flat = level0.reshape(BLOCKS * SHRINK, TRAITS, SAMPLES)
    fold_grams = []
    fold_cross = []
    for fold in range(FOLDS):
        weighted = flat * masks[fold][None, None, :]
        fold_grams.append(jnp.einsum('ats,bts->tab', weighted, flat, precision=HIGH))
        fold_cross.append(jnp.einsum('ats,ts->ta', weighted, traits_wide, precision=HIGH))
    fold_grams = jnp.stack(fold_grams)
    fold_cross = jnp.stack(fold_cross)
    train_grams = lax.optimization_barrier(jnp.sum(fold_grams, axis=0))[None] - fold_grams
    train_cross = lax.optimization_barrier(jnp.sum(fold_cross, axis=0))[None] - fold_cross
    count_pred = BLOCKS * SHRINK
    shrunk = train_grams + SAMPLES / 4.0 * jnp.eye(count_pred, dtype=jnp.float32)
    weights = solve_batch(shrunk.reshape(-1, count_pred, count_pred), train_cross.reshape(-1, count_pred))
    weights = weights.reshape(FOLDS, TRAITS, count_pred)
    every_fold = jnp.einsum('ats,kta->kts', flat, weights, precision=HIGH)
    blended = jnp.einsum('kts,ks->ts', every_fold, masks, precision=HIGH)
    bmean = lax.optimization_barrier(jnp.sum(blended, axis=-1)) / SAMPLES
    bvar = lax.optimization_barrier(jnp.sum(blended * blended, axis=-1)) / SAMPLES - bmean * bmean
    blend = (blended - bmean[:, None]) * lax.rsqrt(bvar + EPS)[:, None]
    return (level0, blend)
```

```python
import jax
import jax.numpy as jnp
import numpy as np
from jax import lax
from jax.sharding import Mesh
from jax.sharding import PartitionSpec as P

FOLDS = 5
SHRINK = 5


RATIOS = (99.0, 3.0, 1.0, 1.0 / 3.0, 1.0 / 99.0)
EPS = 1e-05
HIGH = lax.Precision.HIGHEST
SAMP = ("x", "z", "c")


def solve_batch(systems, right_sides):
    factors = jnp.linalg.cholesky(systems)

    def solve_single(factor, right_side):
        return jax.scipy.linalg.cho_solve((factor, True), right_side)

    return jax.vmap(solve_single)(factors, right_sides)


def psum_tree(value):
    for name in ("c", "z", "x"):
        value = lax.psum(value, name)
    return value


def shards(dosages, traits, folds):
    rows, width = dosages.shape
    traits_count = traits.shape[0]
    fold_ids = jnp.arange(FOLDS, dtype=jnp.int32)
    masks = (folds[None, :] == fold_ids[:, None]).astype(jnp.float32)
    mask_half = masks.astype(jnp.bfloat16)
    traits_wide = traits.astype(jnp.float32)
    augmented = jnp.concatenate(
        [dosages, jnp.ones((rows, 1), jnp.bfloat16), traits.T], axis=1
    )
    weighted = mask_half[:, :, None] * augmented[None]
    stats = jnp.einsum("ri,krj->kij", augmented, weighted, preferred_element_type=jnp.float32)
    stats = lax.psum(stats, SAMP)
    gram = stats[:, :width, :width]
    sums = stats[:, :width, width]
    counts = stats[:, width, width]
    cross = stats[:, width + 1 :, :width]
    trait_sums = stats[:, width + 1 :, width]
    total = jnp.sum(counts)
    mean = jnp.sum(sums, axis=0) / total
    gram_total = jnp.sum(gram, axis=0)
    variance = jnp.diagonal(gram_total) / total - mean * mean
    scale = lax.rsqrt(variance + EPS)
    sums_total = jnp.sum(sums, axis=0)
    cross_total = jnp.sum(cross, axis=0)
    trait_total = jnp.sum(trait_sums, axis=0)
    ratios = jnp.array(RATIOS, dtype=jnp.float32)
    identity = jnp.eye(width, dtype=jnp.float32)

    def train_system(fold):
        train_gram = gram_total - lax.dynamic_index_in_dim(gram, fold, 0, keepdims=False)
        train_sums = sums_total - lax.dynamic_index_in_dim(sums, fold, 0, keepdims=False)
        train_count = total - lax.dynamic_index_in_dim(counts, fold, 0, keepdims=False)
        train_cross = cross_total - lax.dynamic_index_in_dim(cross, fold, 0, keepdims=False)
        train_traits = trait_total - lax.dynamic_index_in_dim(trait_sums, fold, 0, keepdims=False)
        centered = (
            train_gram
            - mean[:, None] * train_sums[None, :]
            - train_sums[:, None] * mean[None, :]
            + train_count * mean[:, None] * mean[None, :]
        )
        system = scale[:, None] * centered * scale[None, :]
        target = scale[:, None] * (train_cross.T - mean[:, None] * train_traits[None, :])
        return (system, target)

    systems_count = FOLDS * SHRINK
    samp_size = lax.axis_size(SAMP)
    per_device = -(-systems_count // samp_size)
    first = lax.axis_index(SAMP) * per_device

    def solve_own(offset):
        which = jnp.minimum(first + offset, systems_count - 1)
        fold = which // SHRINK
        shrink = which - fold * SHRINK
        system, target = train_system(fold)
        penalty = jnp.sum(
            jnp.where(jnp.arange(SHRINK, dtype=jnp.int32) == shrink, ratios * width, 0.0)
        )
        beta = solve_batch((system + penalty * identity)[None], target[None])[0]
        return (scale[:, None] * beta).astype(jnp.bfloat16)

    owned = lax.map(solve_own, jnp.arange(per_device, dtype=jnp.int32))
    collected = lax.all_gather(owned, SAMP, axis=0, tiled=True)
    coef = collected[:systems_count].reshape(FOLDS, SHRINK, width, traits_count)
    coef_flat = coef.transpose(2, 0, 1, 3).reshape(width, FOLDS * SHRINK * traits_count)
    shift = jnp.einsum("v,klvt->klt", mean, coef.astype(jnp.float32), precision=HIGH)
    raw = jnp.einsum("vc,rv->cr", coef_flat, dosages, preferred_element_type=jnp.float32)
    outcome = raw.reshape(FOLDS, SHRINK, traits_count, rows) - shift[..., None]
    level_pred = jnp.einsum("kltr,kr->ltr", outcome, masks, precision=HIGH)
    group = traits_count // lax.axis_size("blk")
    start = lax.axis_index("blk") * group
    own_traits = lax.dynamic_slice_in_dim(traits_wide, start, group, 0)
    own_sums = lax.dynamic_slice_in_dim(trait_sums, start, group, 1)
    arrived = lax.all_to_all(level_pred[None], "blk", split_axis=2, concat_axis=0, tiled=True)
    count_pred = arrived.shape[0] * arrived.shape[1]
    flat = arrived.reshape(count_pred, group, rows)
    raw_grams = jnp.einsum("ks,ats,bts->ktab", masks, flat, flat, precision=HIGH)
    raw_sums = jnp.einsum("ks,ats->kta", masks, flat, precision=HIGH)
    raw_cross = jnp.einsum("ks,ats,ts->kta", masks, flat, own_traits, precision=HIGH)
    packed = jnp.concatenate(
        [raw_grams.reshape(FOLDS * group, count_pred * count_pred),
         raw_sums.reshape(FOLDS * group, count_pred),
         raw_cross.reshape(FOLDS * group, count_pred)],
        axis=1,
    )
    packed = psum_tree(packed)
    raw_grams = packed[:, : count_pred * count_pred].reshape(FOLDS, group, count_pred, count_pred)
    raw_sums = packed[:, count_pred * count_pred : count_pred * (count_pred + 1)].reshape(
        FOLDS, group, count_pred
    )
    raw_cross = packed[:, count_pred * (count_pred + 1) :].reshape(FOLDS, group, count_pred)
    pred_sum = jnp.sum(raw_sums, axis=0)
    pred_sq = jnp.sum(jnp.diagonal(raw_grams, axis1=2, axis2=3), axis=0)
    pred_mean = pred_sum / total
    pred_var = pred_sq / total - pred_mean * pred_mean
    pred_scale = lax.rsqrt(pred_var + EPS)
    level0 = (flat - pred_mean.T[:, :, None]) * pred_scale.T[:, :, None]
    fold_mean = pred_mean[None]
    fold_sums = (raw_sums - counts[:, None, None] * fold_mean) * pred_scale[None]
    fold_grams = (
        raw_grams
        - fold_mean[..., :, None] * raw_sums[..., None, :]
        - raw_sums[..., :, None] * fold_mean[..., None, :]
        + counts[:, None, None, None] * fold_mean[..., :, None] * fold_mean[..., None, :]
    ) * (pred_scale[None, :, :, None] * pred_scale[None, :, None, :])
    fold_cross = (raw_cross - fold_mean * own_sums[:, :, None]) * pred_scale[None]
    level0 = level0.reshape(arrived.shape)
    train_grams = jnp.sum(fold_grams, axis=0)[None] - fold_grams
    train_cross = jnp.sum(fold_cross, axis=0)[None] - fold_cross
    shrunk = train_grams + total / 4.0 * jnp.eye(count_pred, dtype=jnp.float32)
    weights = solve_batch(
        shrunk.reshape(-1, count_pred, count_pred), train_cross.reshape(-1, count_pred)
    )
    weights = weights.reshape(FOLDS, group, count_pred)
    every_fold = jnp.einsum("ats,kta->kts", level0.reshape(flat.shape), weights, precision=HIGH)
    blended = jnp.einsum("kts,ks->ts", every_fold, masks, precision=HIGH)
    blend_sum = jnp.einsum("kta,kta->t", weights, fold_sums, precision=HIGH)
    blend_sq = jnp.einsum("kta,ktab,ktb->t", weights, fold_grams, weights, precision=HIGH)
    blend_mean = blend_sum / total
    blend_var = blend_sq / total - blend_mean * blend_mean
    blend = (blended - blend_mean[:, None]) * lax.rsqrt(blend_var + EPS)[:, None]
    return (level0, blend)


def view_of(mesh):
    devices = np.asarray(mesh.devices)
    samp, blk = devices.shape
    flat = list(devices.reshape(-1))
    xs = sorted({d.coords[0] for d in flat})
    zs = sorted({d.coords[2] for d in flat})
    cores = samp // (len(xs) * len(zs))
    view = devices.reshape(len(xs), len(zs), cores, blk)
    for (i, j, c, b), d in np.ndenumerate(view):
        assert d.coords[0] == xs[i] and d.coords[2] == zs[j]
    return Mesh(view, ("x", "z", "c", "blk"))


def solution(mesh):
    view = view_of(mesh)
    in_specs = (P(SAMP, "blk"), P(None, SAMP), P(SAMP))
    out_specs = (P(None, None, "blk", SAMP), P("blk", SAMP))
    return jax.shard_map(shards, mesh=view, in_specs=in_specs, out_specs=out_specs, check_vma=False)
```

```python
import jax
import jax.numpy as jnp
import numpy as np
from jax import lax
from jax.experimental import pallas as pl
from jax.sharding import Mesh
from jax.sharding import PartitionSpec as P

FOLDS = 5
SHRINK = 5


RATIOS = (99.0, 3.0, 1.0, 1.0 / 3.0, 1.0 / 99.0)
EPS = 1e-05
HIGH = lax.Precision.HIGHEST
SAMP = ("x", "z", "c")


def solve_batch(systems, right_sides):
    factors = jnp.linalg.cholesky(systems)

    def solve_single(factor, right_side):
        return jax.scipy.linalg.cho_solve((factor, True), right_side)

    return jax.vmap(solve_single)(factors, right_sides)


def _cholesky_solve_kernel(a_ref, b_ref, x_ref):
    a = a_ref[...]
    r = b_ref[...]
    n = a.shape[0]
    rows = jax.lax.broadcasted_iota(jnp.int32, r.shape, 0)
    cols = jax.lax.broadcasted_iota(jnp.int32, (1,) + a.shape[1:], 1)
    diags, columns = [], []
    for j in range(n):
        d = jnp.sqrt(a[j : j + 1, j : j + 1, :])
        column = jnp.where(rows >= j, a[:, j : j + 1, :] / d, 0.0)
        row = jnp.where(cols >= j, a[j : j + 1, :, :] / d, 0.0)
        a = a - column * row
        diags.append(d)
        columns.append(column)
    y = jnp.zeros_like(r)
    for j in range(n):
        yj = r[j : j + 1] / diags[j]
        r = r - columns[j] * yj
        y = jnp.where(rows == j, yj, y)
    x = jnp.zeros_like(r)
    for j in reversed(range(n)):
        s = jnp.sum(jnp.where(rows > j, columns[j] * x, 0.0), axis=0, keepdims=True)
        x = jnp.where(rows == j, (y[j : j + 1] - s) / diags[j], x)
    x_ref[...] = x


def cholesky_solve(systems, right_sides):
    batch, n, _ = systems.shape
    a = systems.transpose(1, 2, 0)
    b = right_sides.T[:, None, :]
    x = pl.pallas_call(
        _cholesky_solve_kernel,
        out_shape=jax.ShapeDtypeStruct((n, 1, batch), jnp.float32),
    )(a, b)
    return x[:, 0, :].T


def psum_tree(value):
    for name in ("c", "z", "x"):
        value = lax.psum(value, name)
    return value


def shards(dosages, traits, folds):
    rows, width = dosages.shape
    traits_count = traits.shape[0]
    fold_ids = jnp.arange(FOLDS, dtype=jnp.int32)
    masks = (folds[None, :] == fold_ids[:, None]).astype(jnp.float32)
    mask_half = masks.astype(jnp.bfloat16)
    traits_wide = traits.astype(jnp.float32)
    augmented = jnp.concatenate(
        [dosages, jnp.ones((rows, 1), jnp.bfloat16), traits.T], axis=1
    )
    weighted = mask_half[:, :, None] * augmented[None]
    stats = jnp.einsum("ri,krj->kij", augmented, weighted, preferred_element_type=jnp.float32)
    stats = lax.psum(stats, SAMP)
    gram = stats[:, :width, :width]
    sums = stats[:, :width, width]
    counts = stats[:, width, width]
    cross = stats[:, width + 1 :, :width]
    trait_sums = stats[:, width + 1 :, width]
    total = jnp.sum(counts)
    mean = jnp.sum(sums, axis=0) / total
    gram_total = jnp.sum(gram, axis=0)
    variance = jnp.diagonal(gram_total) / total - mean * mean
    scale = lax.rsqrt(variance + EPS)
    sums_total = jnp.sum(sums, axis=0)
    cross_total = jnp.sum(cross, axis=0)
    trait_total = jnp.sum(trait_sums, axis=0)
    ratios = jnp.array(RATIOS, dtype=jnp.float32)
    identity = jnp.eye(width, dtype=jnp.float32)

    def train_system(fold):
        train_gram = gram_total - lax.dynamic_index_in_dim(gram, fold, 0, keepdims=False)
        train_sums = sums_total - lax.dynamic_index_in_dim(sums, fold, 0, keepdims=False)
        train_count = total - lax.dynamic_index_in_dim(counts, fold, 0, keepdims=False)
        train_cross = cross_total - lax.dynamic_index_in_dim(cross, fold, 0, keepdims=False)
        train_traits = trait_total - lax.dynamic_index_in_dim(trait_sums, fold, 0, keepdims=False)
        centered = (
            train_gram
            - mean[:, None] * train_sums[None, :]
            - train_sums[:, None] * mean[None, :]
            + train_count * mean[:, None] * mean[None, :]
        )
        system = scale[:, None] * centered * scale[None, :]
        target = scale[:, None] * (train_cross.T - mean[:, None] * train_traits[None, :])
        return (system, target)

    systems_count = FOLDS * SHRINK
    samp_size = lax.axis_size(SAMP)
    per_device = -(-systems_count // samp_size)
    first = lax.axis_index(SAMP) * per_device

    def solve_own(offset):
        which = jnp.minimum(first + offset, systems_count - 1)
        fold = which // SHRINK
        shrink = which - fold * SHRINK
        system, target = train_system(fold)
        penalty = jnp.sum(
            jnp.where(jnp.arange(SHRINK, dtype=jnp.int32) == shrink, ratios * width, 0.0)
        )
        beta = solve_batch((system + penalty * identity)[None], target[None])[0]
        return (scale[:, None] * beta).astype(jnp.bfloat16)

    owned = lax.map(solve_own, jnp.arange(per_device, dtype=jnp.int32))
    collected = lax.all_gather(owned, SAMP, axis=0, tiled=True)
    coef = collected[:systems_count].reshape(FOLDS, SHRINK, width, traits_count)
    coef_flat = coef.transpose(2, 0, 1, 3).reshape(width, FOLDS * SHRINK * traits_count)
    shift = jnp.einsum("v,klvt->klt", mean, coef.astype(jnp.float32), precision=HIGH)
    raw = jnp.einsum("vc,rv->cr", coef_flat, dosages, preferred_element_type=jnp.float32)
    outcome = raw.reshape(FOLDS, SHRINK, traits_count, rows) - shift[..., None]
    level_pred = jnp.einsum("kltr,kr->ltr", outcome, masks, precision=HIGH)
    group = traits_count // lax.axis_size("blk")
    start = lax.axis_index("blk") * group
    own_traits = lax.dynamic_slice_in_dim(traits_wide, start, group, 0)
    own_sums = lax.dynamic_slice_in_dim(trait_sums, start, group, 1)
    arrived = lax.all_to_all(level_pred[None], "blk", split_axis=2, concat_axis=0, tiled=True)
    count_pred = arrived.shape[0] * arrived.shape[1]
    flat = arrived.reshape(count_pred, group, rows)
    raw_grams = jnp.einsum("ks,ats,bts->ktab", masks, flat, flat, precision=HIGH)
    raw_sums = jnp.einsum("ks,ats->kta", masks, flat, precision=HIGH)
    raw_cross = jnp.einsum("ks,ats,ts->kta", masks, flat, own_traits, precision=HIGH)
    packed = jnp.concatenate(
        [raw_grams.reshape(FOLDS * group, count_pred * count_pred),
         raw_sums.reshape(FOLDS * group, count_pred),
         raw_cross.reshape(FOLDS * group, count_pred)],
        axis=1,
    )
    packed = psum_tree(packed)
    raw_grams = packed[:, : count_pred * count_pred].reshape(FOLDS, group, count_pred, count_pred)
    raw_sums = packed[:, count_pred * count_pred : count_pred * (count_pred + 1)].reshape(
        FOLDS, group, count_pred
    )
    raw_cross = packed[:, count_pred * (count_pred + 1) :].reshape(FOLDS, group, count_pred)
    pred_sum = jnp.sum(raw_sums, axis=0)
    pred_sq = jnp.sum(jnp.diagonal(raw_grams, axis1=2, axis2=3), axis=0)
    pred_mean = pred_sum / total
    pred_var = pred_sq / total - pred_mean * pred_mean
    pred_scale = lax.rsqrt(pred_var + EPS)
    level0 = (flat - pred_mean.T[:, :, None]) * pred_scale.T[:, :, None]
    fold_mean = pred_mean[None]
    fold_sums = (raw_sums - counts[:, None, None] * fold_mean) * pred_scale[None]
    fold_grams = (
        raw_grams
        - fold_mean[..., :, None] * raw_sums[..., None, :]
        - raw_sums[..., :, None] * fold_mean[..., None, :]
        + counts[:, None, None, None] * fold_mean[..., :, None] * fold_mean[..., None, :]
    ) * (pred_scale[None, :, :, None] * pred_scale[None, :, None, :])
    fold_cross = (raw_cross - fold_mean * own_sums[:, :, None]) * pred_scale[None]
    level0 = level0.reshape(arrived.shape)
    train_grams = jnp.sum(fold_grams, axis=0)[None] - fold_grams
    train_cross = jnp.sum(fold_cross, axis=0)[None] - fold_cross
    shrunk = train_grams + total / 4.0 * jnp.eye(count_pred, dtype=jnp.float32)
    weights = cholesky_solve(
        shrunk.reshape(-1, count_pred, count_pred), train_cross.reshape(-1, count_pred)
    )
    weights = weights.reshape(FOLDS, group, count_pred)
    every_fold = jnp.einsum("ats,kta->kts", level0.reshape(flat.shape), weights, precision=HIGH)
    blended = jnp.einsum("kts,ks->ts", every_fold, masks, precision=HIGH)
    blend_sum = jnp.einsum("kta,kta->t", weights, fold_sums, precision=HIGH)
    blend_sq = jnp.einsum("kta,ktab,ktb->t", weights, fold_grams, weights, precision=HIGH)
    blend_mean = blend_sum / total
    blend_var = blend_sq / total - blend_mean * blend_mean
    blend = (blended - blend_mean[:, None]) * lax.rsqrt(blend_var + EPS)[:, None]
    return (level0, blend)


def view_of(mesh):
    devices = np.asarray(mesh.devices)
    samp, blk = devices.shape
    flat = list(devices.reshape(-1))
    xs = sorted({d.coords[0] for d in flat})
    zs = sorted({d.coords[2] for d in flat})
    cores = samp // (len(xs) * len(zs))
    view = devices.reshape(len(xs), len(zs), cores, blk)
    for (i, j, c, b), d in np.ndenumerate(view):
        assert d.coords[0] == xs[i] and d.coords[2] == zs[j]
    return Mesh(view, ("x", "z", "c", "blk"))


def solution(mesh):
    view = view_of(mesh)
    in_specs = (P(SAMP, "blk"), P(None, SAMP), P(SAMP))
    out_specs = (P(None, None, "blk", SAMP), P("blk", SAMP))
    return jax.shard_map(shards, mesh=view, in_specs=in_specs, out_specs=out_specs, check_vma=False)
```

```python
import jax
import jax.numpy as jnp
import numpy as np
from jax import lax
from jax.experimental import pallas as pl
from jax.sharding import Mesh
from jax.sharding import PartitionSpec as P

FOLDS = 5
SHRINK = 5


RATIOS = (99.0, 3.0, 1.0, 1.0 / 3.0, 1.0 / 99.0)
EPS = 1e-05
HIGH = lax.Precision.HIGHEST
SAMP = ("x", "z", "c")


def solve_batch(systems, right_sides):
    factors = jnp.linalg.cholesky(systems)

    def solve_single(factor, right_side):
        return jax.scipy.linalg.cho_solve((factor, True), right_side)

    return jax.vmap(solve_single)(factors, right_sides)


def _cholesky_solve_kernel(a_ref, b_ref, x_ref):
    a = a_ref[...]
    r = b_ref[...]
    n = a.shape[0]
    rows = jax.lax.broadcasted_iota(jnp.int32, r.shape, 0)
    cols = jax.lax.broadcasted_iota(jnp.int32, (1,) + a.shape[1:], 1)
    diags, columns = [], []
    for j in range(n):
        d = jnp.sqrt(a[j : j + 1, j : j + 1, :])
        column = jnp.where(rows >= j, a[:, j : j + 1, :] / d, 0.0)
        row = jnp.where(cols >= j, a[j : j + 1, :, :] / d, 0.0)
        a = a - column * row
        diags.append(d)
        columns.append(column)
    y = jnp.zeros_like(r)
    for j in range(n):
        yj = r[j : j + 1] / diags[j]
        r = r - columns[j] * yj
        y = jnp.where(rows == j, yj, y)
    x = jnp.zeros_like(r)
    for j in reversed(range(n)):
        s = jnp.sum(jnp.where(rows > j, columns[j] * x, 0.0), axis=0, keepdims=True)
        x = jnp.where(rows == j, (y[j : j + 1] - s) / diags[j], x)
    x_ref[...] = x


def cholesky_solve(systems, right_sides):
    batch, n, _ = systems.shape
    a = systems.transpose(1, 2, 0)
    b = right_sides.T[:, None, :]
    x = pl.pallas_call(
        _cholesky_solve_kernel,
        out_shape=jax.ShapeDtypeStruct((n, 1, batch), jnp.float32),
    )(a, b)
    return x[:, 0, :].T


def psum_tree(value):
    for name in ("c", "z", "x"):
        value = lax.psum(value, name)
    return value


def shards(dosages, traits, folds):
    rows, width = dosages.shape
    traits_count = traits.shape[0]
    fold_ids = jnp.arange(FOLDS, dtype=jnp.int32)
    masks = (folds[None, :] == fold_ids[:, None]).astype(jnp.float32)
    mask_half = masks.astype(jnp.bfloat16)
    traits_wide = traits.astype(jnp.float32)
    augmented = jnp.concatenate(
        [dosages, jnp.ones((rows, 1), jnp.bfloat16), traits.T], axis=1
    )
    weighted = mask_half[:, :, None] * augmented[None]
    stats = jnp.einsum("ri,krj->kij", augmented, weighted, preferred_element_type=jnp.float32)
    stats = lax.psum(stats, SAMP)
    gram = stats[:, :width, :width]
    sums = stats[:, :width, width]
    counts = stats[:, width, width]
    cross = stats[:, width + 1 :, :width]
    trait_sums = stats[:, width + 1 :, width]
    total = jnp.sum(counts)
    mean = jnp.sum(sums, axis=0) / total
    gram_total = jnp.sum(gram, axis=0)
    variance = jnp.diagonal(gram_total) / total - mean * mean
    scale = lax.rsqrt(variance + EPS)
    sums_total = jnp.sum(sums, axis=0)
    cross_total = jnp.sum(cross, axis=0)
    trait_total = jnp.sum(trait_sums, axis=0)
    ratios = jnp.array(RATIOS, dtype=jnp.float32)
    identity = jnp.eye(width, dtype=jnp.float32)

    def train_system(fold):
        train_gram = gram_total - lax.dynamic_index_in_dim(gram, fold, 0, keepdims=False)
        train_sums = sums_total - lax.dynamic_index_in_dim(sums, fold, 0, keepdims=False)
        train_count = total - lax.dynamic_index_in_dim(counts, fold, 0, keepdims=False)
        train_cross = cross_total - lax.dynamic_index_in_dim(cross, fold, 0, keepdims=False)
        train_traits = trait_total - lax.dynamic_index_in_dim(trait_sums, fold, 0, keepdims=False)
        centered = (
            train_gram
            - mean[:, None] * train_sums[None, :]
            - train_sums[:, None] * mean[None, :]
            + train_count * mean[:, None] * mean[None, :]
        )
        system = scale[:, None] * centered * scale[None, :]
        target = scale[:, None] * (train_cross.T - mean[:, None] * train_traits[None, :])
        return (system, target)

    systems_count = FOLDS * SHRINK
    slots = lax.axis_size(("x", "z"))
    per_device = -(-systems_count // slots)
    first = lax.axis_index(("x", "z")) * per_device

    def solve_own(offset):
        which = jnp.minimum(first + offset, systems_count - 1)
        fold = which // SHRINK
        shrink = which - fold * SHRINK
        system, target = train_system(fold)
        penalty = jnp.sum(
            jnp.where(jnp.arange(SHRINK, dtype=jnp.int32) == shrink, ratios * width, 0.0)
        )
        beta = solve_batch((system + penalty * identity)[None], target[None])[0]
        return (scale[:, None] * beta).astype(jnp.bfloat16)

    owned = lax.map(solve_own, jnp.arange(per_device, dtype=jnp.int32))
    collected = lax.all_gather(owned, "z", axis=0, tiled=True)
    collected = lax.all_gather(collected, "x", axis=0, tiled=True)
    coef = collected[:systems_count].reshape(FOLDS, SHRINK, width, traits_count)
    coef_flat = coef.transpose(2, 0, 1, 3).reshape(width, FOLDS * SHRINK * traits_count)
    shift = jnp.einsum("v,klvt->klt", mean, coef.astype(jnp.float32), precision=HIGH)
    raw = jnp.einsum("vc,rv->cr", coef_flat, dosages, preferred_element_type=jnp.float32)
    outcome = raw.reshape(FOLDS, SHRINK, traits_count, rows) - shift[..., None]
    level_pred = jnp.einsum("kltr,kr->ltr", outcome, masks, precision=HIGH)
    group = traits_count // lax.axis_size("blk")
    start = lax.axis_index("blk") * group
    own_traits = lax.dynamic_slice_in_dim(traits_wide, start, group, 0)
    own_sums = lax.dynamic_slice_in_dim(trait_sums, start, group, 1)
    arrived = lax.all_to_all(level_pred[None], "blk", split_axis=2, concat_axis=0, tiled=True)
    count_pred = arrived.shape[0] * arrived.shape[1]
    flat = arrived.reshape(count_pred, group, rows)
    raw_grams = jnp.einsum("ks,ats,bts->ktab", masks, flat, flat, precision=HIGH)
    raw_sums = jnp.einsum("ks,ats->kta", masks, flat, precision=HIGH)
    raw_cross = jnp.einsum("ks,ats,ts->kta", masks, flat, own_traits, precision=HIGH)
    packed = jnp.concatenate(
        [raw_grams.reshape(FOLDS * group, count_pred * count_pred),
         raw_sums.reshape(FOLDS * group, count_pred),
         raw_cross.reshape(FOLDS * group, count_pred)],
        axis=1,
    )
    packed = psum_tree(packed)
    raw_grams = packed[:, : count_pred * count_pred].reshape(FOLDS, group, count_pred, count_pred)
    raw_sums = packed[:, count_pred * count_pred : count_pred * (count_pred + 1)].reshape(
        FOLDS, group, count_pred
    )
    raw_cross = packed[:, count_pred * (count_pred + 1) :].reshape(FOLDS, group, count_pred)
    pred_sum = jnp.sum(raw_sums, axis=0)
    pred_sq = jnp.sum(jnp.diagonal(raw_grams, axis1=2, axis2=3), axis=0)
    pred_mean = pred_sum / total
    pred_var = pred_sq / total - pred_mean * pred_mean
    pred_scale = lax.rsqrt(pred_var + EPS)
    level0 = (flat - pred_mean.T[:, :, None]) * pred_scale.T[:, :, None]
    fold_mean = pred_mean[None]
    fold_sums = (raw_sums - counts[:, None, None] * fold_mean) * pred_scale[None]
    fold_grams = (
        raw_grams
        - fold_mean[..., :, None] * raw_sums[..., None, :]
        - raw_sums[..., :, None] * fold_mean[..., None, :]
        + counts[:, None, None, None] * fold_mean[..., :, None] * fold_mean[..., None, :]
    ) * (pred_scale[None, :, :, None] * pred_scale[None, :, None, :])
    fold_cross = (raw_cross - fold_mean * own_sums[:, :, None]) * pred_scale[None]
    level0 = level0.reshape(arrived.shape)
    train_grams = jnp.sum(fold_grams, axis=0)[None] - fold_grams
    train_cross = jnp.sum(fold_cross, axis=0)[None] - fold_cross
    shrunk = train_grams + total / 4.0 * jnp.eye(count_pred, dtype=jnp.float32)
    weights = cholesky_solve(
        shrunk.reshape(-1, count_pred, count_pred), train_cross.reshape(-1, count_pred)
    )
    weights = weights.reshape(FOLDS, group, count_pred)
    every_fold = jnp.einsum("ats,kta->kts", level0.reshape(flat.shape), weights, precision=HIGH)
    blended = jnp.einsum("kts,ks->ts", every_fold, masks, precision=HIGH)
    blend_sum = jnp.einsum("kta,kta->t", weights, fold_sums, precision=HIGH)
    blend_sq = jnp.einsum("kta,ktab,ktb->t", weights, fold_grams, weights, precision=HIGH)
    blend_mean = blend_sum / total
    blend_var = blend_sq / total - blend_mean * blend_mean
    blend = (blended - blend_mean[:, None]) * lax.rsqrt(blend_var + EPS)[:, None]
    return (level0, blend)


def view_of(mesh):
    devices = np.asarray(mesh.devices)
    samp, blk = devices.shape
    flat = list(devices.reshape(-1))
    xs = sorted({d.coords[0] for d in flat})
    zs = sorted({d.coords[2] for d in flat})
    cores = samp // (len(xs) * len(zs))
    view = devices.reshape(len(xs), len(zs), cores, blk)
    for (i, j, c, b), d in np.ndenumerate(view):
        assert d.coords[0] == xs[i] and d.coords[2] == zs[j]
    return Mesh(view, ("x", "z", "c", "blk"))


def solution(mesh):
    view = view_of(mesh)
    in_specs = (P(SAMP, "blk"), P(None, SAMP), P(SAMP))
    out_specs = (P(None, None, "blk", SAMP), P("blk", SAMP))
    return jax.shard_map(shards, mesh=view, in_specs=in_specs, out_specs=out_specs, check_vma=False)
```

```python
import jax
import jax.numpy as jnp
import numpy as np
from jax import lax
from jax.experimental import pallas as pl
from jax.sharding import Mesh
from jax.sharding import PartitionSpec as P

FOLDS = 5
SHRINK = 5


RATIOS = (99.0, 3.0, 1.0, 1.0 / 3.0, 1.0 / 99.0)
EPS = 1e-05
HIGH = lax.Precision.HIGHEST
SAMP = ("x", "z", "c")


def solve_batch(systems, right_sides):
    factors = jnp.linalg.cholesky(systems)

    def solve_single(factor, right_side):
        return jax.scipy.linalg.cho_solve((factor, True), right_side)

    return jax.vmap(solve_single)(factors, right_sides)


def _cholesky_solve_kernel(a_ref, b_ref, x_ref):
    a = a_ref[...]
    r = b_ref[...]
    n = a.shape[0]
    rows = jax.lax.broadcasted_iota(jnp.int32, r.shape, 0)
    cols = jax.lax.broadcasted_iota(jnp.int32, (1,) + a.shape[1:], 1)
    diags, columns = [], []
    for j in range(n):
        d = jnp.sqrt(a[j : j + 1, j : j + 1, :])
        column = jnp.where(rows >= j, a[:, j : j + 1, :] / d, 0.0)
        row = jnp.where(cols >= j, a[j : j + 1, :, :] / d, 0.0)
        a = a - column * row
        diags.append(d)
        columns.append(column)
    y = jnp.zeros_like(r)
    for j in range(n):
        yj = r[j : j + 1] / diags[j]
        r = r - columns[j] * yj
        y = jnp.where(rows == j, yj, y)
    x = jnp.zeros_like(r)
    for j in reversed(range(n)):
        s = jnp.sum(jnp.where(rows > j, columns[j] * x, 0.0), axis=0, keepdims=True)
        x = jnp.where(rows == j, (y[j : j + 1] - s) / diags[j], x)
    x_ref[...] = x


def cholesky_solve(systems, right_sides):
    batch, n, _ = systems.shape
    a = systems.transpose(1, 2, 0)
    b = right_sides.T[:, None, :]
    x = pl.pallas_call(
        _cholesky_solve_kernel,
        out_shape=jax.ShapeDtypeStruct((n, 1, batch), jnp.float32),
    )(a, b)
    return x[:, 0, :].T


def psum_tree(value):
    for name in ("c", "z", "x"):
        value = lax.psum(value, name)
    return value


def reduce_scatter_a2a(value, name):
    n = lax.axis_size(name)
    value = value.reshape((n, value.shape[0] // n) + value.shape[1:])
    return jnp.sum(lax.all_to_all(value, name, 0, 0, tiled=True), axis=0)


def psum_symmetric(stats):
    count, size, _ = stats.shape
    upper = jnp.triu(jnp.ones((size, size), jnp.bool_))
    pairs = count // 2
    packed = [jnp.where(upper, stats[2 * i], stats[2 * i + 1]) for i in range(pairs)]
    packed += [stats[i] for i in range(2 * pairs, count)]
    diagonals = [jnp.diagonal(stats[2 * i + 1])[None] for i in range(pairs)]
    rows = jnp.concatenate([p for p in packed] + diagonals, axis=0)
    parts = lax.axis_size(SAMP)
    padded = -(-rows.shape[0] // parts) * parts
    rows = jnp.pad(rows, ((0, padded - rows.shape[0]), (0, 0)))
    for name in ("c", "z", "x"):
        rows = reduce_scatter_a2a(rows, name)
    for name in ("x", "z", "c"):
        rows = lax.all_gather(rows, name, axis=0, tiled=True)
    squares = len(packed)
    blocks = rows[: squares * size].reshape(squares, size, size)
    diagonals = rows[squares * size : squares * size + pairs]
    eye = jnp.eye(size, dtype=jnp.bool_)
    out = []
    for i in range(pairs):
        block = blocks[i]
        first = jnp.where(upper, block, block.T)
        second = jnp.where(eye, diagonals[i][None, :], jnp.where(upper, block.T, block))
        out += [first, second]
    out += [blocks[i] for i in range(pairs, squares)]
    return jnp.stack(out)


def shards(dosages, traits, folds):
    rows, width = dosages.shape
    traits_count = traits.shape[0]
    fold_ids = jnp.arange(FOLDS, dtype=jnp.int32)
    masks = (folds[None, :] == fold_ids[:, None]).astype(jnp.float32)
    mask_half = masks.astype(jnp.bfloat16)
    traits_wide = traits.astype(jnp.float32)
    augmented = jnp.concatenate(
        [dosages, jnp.ones((rows, 1), jnp.bfloat16), traits.T], axis=1
    )
    weighted = mask_half[:, :, None] * augmented[None]
    stats = jnp.einsum("ri,krj->kij", augmented, weighted, preferred_element_type=jnp.float32)
    stats = psum_symmetric(stats)
    gram = stats[:, :width, :width]
    sums = stats[:, :width, width]
    counts = stats[:, width, width]
    cross = stats[:, width + 1 :, :width]
    trait_sums = stats[:, width + 1 :, width]
    total = jnp.sum(counts)
    mean = jnp.sum(sums, axis=0) / total
    gram_total = jnp.sum(gram, axis=0)
    variance = jnp.diagonal(gram_total) / total - mean * mean
    scale = lax.rsqrt(variance + EPS)
    sums_total = jnp.sum(sums, axis=0)
    cross_total = jnp.sum(cross, axis=0)
    trait_total = jnp.sum(trait_sums, axis=0)
    ratios = jnp.array(RATIOS, dtype=jnp.float32)
    identity = jnp.eye(width, dtype=jnp.float32)

    def train_system(fold):
        train_gram = gram_total - lax.dynamic_index_in_dim(gram, fold, 0, keepdims=False)
        train_sums = sums_total - lax.dynamic_index_in_dim(sums, fold, 0, keepdims=False)
        train_count = total - lax.dynamic_index_in_dim(counts, fold, 0, keepdims=False)
        train_cross = cross_total - lax.dynamic_index_in_dim(cross, fold, 0, keepdims=False)
        train_traits = trait_total - lax.dynamic_index_in_dim(trait_sums, fold, 0, keepdims=False)
        centered = (
            train_gram
            - mean[:, None] * train_sums[None, :]
            - train_sums[:, None] * mean[None, :]
            + train_count * mean[:, None] * mean[None, :]
        )
        system = scale[:, None] * centered * scale[None, :]
        target = scale[:, None] * (train_cross.T - mean[:, None] * train_traits[None, :])
        return (system, target)

    systems_count = FOLDS * SHRINK
    slots = lax.axis_size(("x", "z"))
    per_device = -(-systems_count // slots)
    first = lax.axis_index(("x", "z")) * per_device

    def solve_own(offset):
        which = jnp.minimum(first + offset, systems_count - 1)
        fold = which // SHRINK
        shrink = which - fold * SHRINK
        system, target = train_system(fold)
        penalty = jnp.sum(
            jnp.where(jnp.arange(SHRINK, dtype=jnp.int32) == shrink, ratios * width, 0.0)
        )
        beta = solve_batch((system + penalty * identity)[None], target[None])[0]
        return (scale[:, None] * beta).astype(jnp.bfloat16)

    owned = lax.map(solve_own, jnp.arange(per_device, dtype=jnp.int32))
    collected = lax.all_gather(owned, "z", axis=0, tiled=True)
    collected = lax.all_gather(collected, "x", axis=0, tiled=True)
    coef = collected[:systems_count].reshape(FOLDS, SHRINK, width, traits_count)
    coef_flat = coef.transpose(2, 0, 1, 3).reshape(width, FOLDS * SHRINK * traits_count)
    shift = jnp.einsum("v,klvt->klt", mean, coef.astype(jnp.float32), precision=HIGH)
    raw = jnp.einsum("vc,rv->cr", coef_flat, dosages, preferred_element_type=jnp.float32)
    outcome = raw.reshape(FOLDS, SHRINK, traits_count, rows) - shift[..., None]
    level_pred = jnp.einsum("kltr,kr->ltr", outcome, masks, precision=HIGH)
    group = traits_count // lax.axis_size("blk")
    start = lax.axis_index("blk") * group
    own_traits = lax.dynamic_slice_in_dim(traits_wide, start, group, 0)
    own_sums = lax.dynamic_slice_in_dim(trait_sums, start, group, 1)
    arrived = lax.all_to_all(level_pred[None], "blk", split_axis=2, concat_axis=0, tiled=True)
    count_pred = arrived.shape[0] * arrived.shape[1]
    flat = arrived.reshape(count_pred, group, rows)
    raw_grams = jnp.einsum("ks,ats,bts->ktab", masks, flat, flat, precision=HIGH)
    raw_sums = jnp.einsum("ks,ats->kta", masks, flat, precision=HIGH)
    raw_cross = jnp.einsum("ks,ats,ts->kta", masks, flat, own_traits, precision=HIGH)
    packed = jnp.concatenate(
        [raw_grams.reshape(FOLDS * group, count_pred * count_pred),
         raw_sums.reshape(FOLDS * group, count_pred),
         raw_cross.reshape(FOLDS * group, count_pred)],
        axis=1,
    )
    packed = psum_tree(packed)
    raw_grams = packed[:, : count_pred * count_pred].reshape(FOLDS, group, count_pred, count_pred)
    raw_sums = packed[:, count_pred * count_pred : count_pred * (count_pred + 1)].reshape(
        FOLDS, group, count_pred
    )
    raw_cross = packed[:, count_pred * (count_pred + 1) :].reshape(FOLDS, group, count_pred)
    pred_sum = jnp.sum(raw_sums, axis=0)
    pred_sq = jnp.sum(jnp.diagonal(raw_grams, axis1=2, axis2=3), axis=0)
    pred_mean = pred_sum / total
    pred_var = pred_sq / total - pred_mean * pred_mean
    pred_scale = lax.rsqrt(pred_var + EPS)
    level0 = (flat - pred_mean.T[:, :, None]) * pred_scale.T[:, :, None]
    fold_mean = pred_mean[None]
    fold_sums = (raw_sums - counts[:, None, None] * fold_mean) * pred_scale[None]
    fold_grams = (
        raw_grams
        - fold_mean[..., :, None] * raw_sums[..., None, :]
        - raw_sums[..., :, None] * fold_mean[..., None, :]
        + counts[:, None, None, None] * fold_mean[..., :, None] * fold_mean[..., None, :]
    ) * (pred_scale[None, :, :, None] * pred_scale[None, :, None, :])
    fold_cross = (raw_cross - fold_mean * own_sums[:, :, None]) * pred_scale[None]
    level0 = level0.reshape(arrived.shape)
    train_grams = jnp.sum(fold_grams, axis=0)[None] - fold_grams
    train_cross = jnp.sum(fold_cross, axis=0)[None] - fold_cross
    shrunk = train_grams + total / 4.0 * jnp.eye(count_pred, dtype=jnp.float32)
    weights = cholesky_solve(
        shrunk.reshape(-1, count_pred, count_pred), train_cross.reshape(-1, count_pred)
    )
    weights = weights.reshape(FOLDS, group, count_pred)
    every_fold = jnp.einsum("ats,kta->kts", level0.reshape(flat.shape), weights, precision=HIGH)
    blended = jnp.einsum("kts,ks->ts", every_fold, masks, precision=HIGH)
    blend_sum = jnp.einsum("kta,kta->t", weights, fold_sums, precision=HIGH)
    blend_sq = jnp.einsum("kta,ktab,ktb->t", weights, fold_grams, weights, precision=HIGH)
    blend_mean = blend_sum / total
    blend_var = blend_sq / total - blend_mean * blend_mean
    blend = (blended - blend_mean[:, None]) * lax.rsqrt(blend_var + EPS)[:, None]
    return (level0, blend)


def view_of(mesh):
    devices = np.asarray(mesh.devices)
    samp, blk = devices.shape
    flat = list(devices.reshape(-1))
    xs = sorted({d.coords[0] for d in flat})
    zs = sorted({d.coords[2] for d in flat})
    cores = samp // (len(xs) * len(zs))
    view = devices.reshape(len(xs), len(zs), cores, blk)
    for (i, j, c, b), d in np.ndenumerate(view):
        assert d.coords[0] == xs[i] and d.coords[2] == zs[j]
    return Mesh(view, ("x", "z", "c", "blk"))


def solution(mesh):
    view = view_of(mesh)
    in_specs = (P(SAMP, "blk"), P(None, SAMP), P(SAMP))
    out_specs = (P(None, None, "blk", SAMP), P("blk", SAMP))
    return jax.shard_map(shards, mesh=view, in_specs=in_specs, out_specs=out_specs, check_vma=False)
```

```python
import jax
import jax.numpy as jnp
import numpy as np
from jax import lax
from jax.experimental import pallas as pl
from jax.sharding import Mesh
from jax.sharding import PartitionSpec as P

FOLDS = 5
SHRINK = 5


RATIOS = (99.0, 3.0, 1.0, 1.0 / 3.0, 1.0 / 99.0)
EPS = 1e-05
HIGH = lax.Precision.HIGHEST
SAMP = ("x", "z", "c")


def solve_batch(systems, right_sides):
    factors = jnp.linalg.cholesky(systems)

    def solve_single(factor, right_side):
        return jax.scipy.linalg.cho_solve((factor, True), right_side)

    return jax.vmap(solve_single)(factors, right_sides)


def _cholesky_solve_kernel(a_ref, b_ref, x_ref):
    a = a_ref[...]
    r = b_ref[...]
    n = a.shape[0]
    rows = jax.lax.broadcasted_iota(jnp.int32, r.shape, 0)
    cols = jax.lax.broadcasted_iota(jnp.int32, (1,) + a.shape[1:], 1)
    diags, columns = [], []
    for j in range(n):
        d = jnp.sqrt(a[j : j + 1, j : j + 1, :])
        column = jnp.where(rows >= j, a[:, j : j + 1, :] / d, 0.0)
        row = jnp.where(cols >= j, a[j : j + 1, :, :] / d, 0.0)
        a = a - column * row
        diags.append(d)
        columns.append(column)
    y = jnp.zeros_like(r)
    for j in range(n):
        yj = r[j : j + 1] / diags[j]
        r = r - columns[j] * yj
        y = jnp.where(rows == j, yj, y)
    x = jnp.zeros_like(r)
    for j in reversed(range(n)):
        s = jnp.sum(jnp.where(rows > j, columns[j] * x, 0.0), axis=0, keepdims=True)
        x = jnp.where(rows == j, (y[j : j + 1] - s) / diags[j], x)
    x_ref[...] = x


def cholesky_solve(systems, right_sides):
    batch, n, _ = systems.shape
    a = systems.transpose(1, 2, 0)
    b = right_sides.T[:, None, :]
    x = pl.pallas_call(
        _cholesky_solve_kernel,
        out_shape=jax.ShapeDtypeStruct((n, 1, batch), jnp.float32),
    )(a, b)
    return x[:, 0, :].T


def gather_a2a(value, name):
    n = lax.axis_size(name)
    copies = jnp.broadcast_to(value[None], (n,) + value.shape)
    return lax.all_to_all(copies, name, 0, 0, tiled=True)


def psum_tree(value):
    value = lax.psum(value, "c")
    for name in ("z", "x"):
        value = jnp.sum(gather_a2a(value, name), axis=0)
    return value


def shards(dosages, traits, folds):
    rows, width = dosages.shape
    traits_count = traits.shape[0]
    fold_ids = jnp.arange(FOLDS, dtype=jnp.int32)
    masks = (folds[None, :] == fold_ids[:, None]).astype(jnp.float32)
    mask_half = masks.astype(jnp.bfloat16)
    traits_wide = traits.astype(jnp.float32)
    augmented = jnp.concatenate(
        [dosages, jnp.ones((rows, 1), jnp.bfloat16), traits.T], axis=1
    )
    weighted = mask_half[:, :, None] * augmented[None]
    stats = jnp.einsum("ri,krj->kij", augmented, weighted, preferred_element_type=jnp.float32)
    stats = lax.psum(stats, SAMP)
    gram = stats[:, :width, :width]
    sums = stats[:, :width, width]
    counts = stats[:, width, width]
    cross = stats[:, width + 1 :, :width]
    trait_sums = stats[:, width + 1 :, width]
    total = jnp.sum(counts)
    mean = jnp.sum(sums, axis=0) / total
    gram_total = jnp.sum(gram, axis=0)
    variance = jnp.diagonal(gram_total) / total - mean * mean
    scale = lax.rsqrt(variance + EPS)
    sums_total = jnp.sum(sums, axis=0)
    cross_total = jnp.sum(cross, axis=0)
    trait_total = jnp.sum(trait_sums, axis=0)
    ratios = jnp.array(RATIOS, dtype=jnp.float32)
    identity = jnp.eye(width, dtype=jnp.float32)

    def train_system(fold):
        train_gram = gram_total - lax.dynamic_index_in_dim(gram, fold, 0, keepdims=False)
        train_sums = sums_total - lax.dynamic_index_in_dim(sums, fold, 0, keepdims=False)
        train_count = total - lax.dynamic_index_in_dim(counts, fold, 0, keepdims=False)
        train_cross = cross_total - lax.dynamic_index_in_dim(cross, fold, 0, keepdims=False)
        train_traits = trait_total - lax.dynamic_index_in_dim(trait_sums, fold, 0, keepdims=False)
        centered = (
            train_gram
            - mean[:, None] * train_sums[None, :]
            - train_sums[:, None] * mean[None, :]
            + train_count * mean[:, None] * mean[None, :]
        )
        system = scale[:, None] * centered * scale[None, :]
        target = scale[:, None] * (train_cross.T - mean[:, None] * train_traits[None, :])
        return (system, target)

    systems_count = FOLDS * SHRINK
    slots = lax.axis_size(("x", "z"))
    per_device = -(-systems_count // slots)
    first = lax.axis_index(("x", "z")) * per_device

    def solve_own(offset):
        which = jnp.minimum(first + offset, systems_count - 1)
        fold = which // SHRINK
        shrink = which - fold * SHRINK
        system, target = train_system(fold)
        penalty = jnp.sum(
            jnp.where(jnp.arange(SHRINK, dtype=jnp.int32) == shrink, ratios * width, 0.0)
        )
        beta = solve_batch((system + penalty * identity)[None], target[None])[0]
        return (scale[:, None] * beta).astype(jnp.bfloat16)

    owned = lax.map(solve_own, jnp.arange(per_device, dtype=jnp.int32))
    collected = gather_a2a(owned, "z")
    collected = gather_a2a(collected.reshape((-1,) + owned.shape[1:]), "x")
    collected = collected.reshape((-1,) + owned.shape[1:])
    coef = collected[:systems_count].reshape(FOLDS, SHRINK, width, traits_count)
    coef_flat = coef.transpose(2, 0, 1, 3).reshape(width, FOLDS * SHRINK * traits_count)
    shift = jnp.einsum("v,klvt->klt", mean, coef.astype(jnp.float32), precision=HIGH)
    raw = jnp.einsum("vc,rv->cr", coef_flat, dosages, preferred_element_type=jnp.float32)
    outcome = raw.reshape(FOLDS, SHRINK, traits_count, rows) - shift[..., None]
    level_pred = jnp.einsum("kltr,kr->ltr", outcome, masks, precision=HIGH)
    group = traits_count // lax.axis_size("blk")
    start = lax.axis_index("blk") * group
    own_traits = lax.dynamic_slice_in_dim(traits_wide, start, group, 0)
    own_sums = lax.dynamic_slice_in_dim(trait_sums, start, group, 1)
    arrived = lax.all_to_all(level_pred[None], "blk", split_axis=2, concat_axis=0, tiled=True)
    count_pred = arrived.shape[0] * arrived.shape[1]
    flat = arrived.reshape(count_pred, group, rows)
    raw_grams = jnp.einsum("ks,ats,bts->ktab", masks, flat, flat, precision=HIGH)
    raw_sums = jnp.einsum("ks,ats->kta", masks, flat, precision=HIGH)
    raw_cross = jnp.einsum("ks,ats,ts->kta", masks, flat, own_traits, precision=HIGH)
    packed = jnp.concatenate(
        [raw_grams.reshape(FOLDS * group, count_pred * count_pred),
         raw_sums.reshape(FOLDS * group, count_pred),
         raw_cross.reshape(FOLDS * group, count_pred)],
        axis=1,
    )
    packed = psum_tree(packed)
    raw_grams = packed[:, : count_pred * count_pred].reshape(FOLDS, group, count_pred, count_pred)
    raw_sums = packed[:, count_pred * count_pred : count_pred * (count_pred + 1)].reshape(
        FOLDS, group, count_pred
    )
    raw_cross = packed[:, count_pred * (count_pred + 1) :].reshape(FOLDS, group, count_pred)
    pred_sum = jnp.sum(raw_sums, axis=0)
    pred_sq = jnp.sum(jnp.diagonal(raw_grams, axis1=2, axis2=3), axis=0)
    pred_mean = pred_sum / total
    pred_var = pred_sq / total - pred_mean * pred_mean
    pred_scale = lax.rsqrt(pred_var + EPS)
    level0 = (flat - pred_mean.T[:, :, None]) * pred_scale.T[:, :, None]
    fold_mean = pred_mean[None]
    fold_sums = (raw_sums - counts[:, None, None] * fold_mean) * pred_scale[None]
    fold_grams = (
        raw_grams
        - fold_mean[..., :, None] * raw_sums[..., None, :]
        - raw_sums[..., :, None] * fold_mean[..., None, :]
        + counts[:, None, None, None] * fold_mean[..., :, None] * fold_mean[..., None, :]
    ) * (pred_scale[None, :, :, None] * pred_scale[None, :, None, :])
    fold_cross = (raw_cross - fold_mean * own_sums[:, :, None]) * pred_scale[None]
    level0 = level0.reshape(arrived.shape)
    train_grams = jnp.sum(fold_grams, axis=0)[None] - fold_grams
    train_cross = jnp.sum(fold_cross, axis=0)[None] - fold_cross
    shrunk = train_grams + total / 4.0 * jnp.eye(count_pred, dtype=jnp.float32)
    weights = cholesky_solve(
        shrunk.reshape(-1, count_pred, count_pred), train_cross.reshape(-1, count_pred)
    )
    weights = weights.reshape(FOLDS, group, count_pred)
    every_fold = jnp.einsum("ats,kta->kts", level0.reshape(flat.shape), weights, precision=HIGH)
    blended = jnp.einsum("kts,ks->ts", every_fold, masks, precision=HIGH)
    blend_sum = jnp.einsum("kta,kta->t", weights, fold_sums, precision=HIGH)
    blend_sq = jnp.einsum("kta,ktab,ktb->t", weights, fold_grams, weights, precision=HIGH)
    blend_mean = blend_sum / total
    blend_var = blend_sq / total - blend_mean * blend_mean
    blend = (blended - blend_mean[:, None]) * lax.rsqrt(blend_var + EPS)[:, None]
    return (level0, blend)


def view_of(mesh):
    devices = np.asarray(mesh.devices)
    samp, blk = devices.shape
    flat = list(devices.reshape(-1))
    xs = sorted({d.coords[0] for d in flat})
    zs = sorted({d.coords[2] for d in flat})
    cores = samp // (len(xs) * len(zs))
    view = devices.reshape(len(xs), len(zs), cores, blk)
    for (i, j, c, b), d in np.ndenumerate(view):
        assert d.coords[0] == xs[i] and d.coords[2] == zs[j]
    return Mesh(view, ("x", "z", "c", "blk"))


def solution(mesh):
    view = view_of(mesh)
    in_specs = (P(SAMP, "blk"), P(None, SAMP), P(SAMP))
    out_specs = (P(None, None, "blk", SAMP), P("blk", SAMP))
    return jax.shard_map(shards, mesh=view, in_specs=in_specs, out_specs=out_specs, check_vma=False)
```

```python
import jax
import jax.numpy as jnp
import numpy as np
from jax import lax
from jax.experimental import pallas as pl
from jax.sharding import Mesh
from jax.sharding import PartitionSpec as P

FOLDS = 5
SHRINK = 5


RATIOS = (99.0, 3.0, 1.0, 1.0 / 3.0, 1.0 / 99.0)
EPS = 1e-05
HIGH = lax.Precision.HIGHEST
SAMP = ("x", "z", "c")


def solve_batch(systems, right_sides):
    factors = jnp.linalg.cholesky(systems)

    def solve_single(factor, right_side):
        return jax.scipy.linalg.cho_solve((factor, True), right_side)

    return jax.vmap(solve_single)(factors, right_sides)


def blocked_cholesky_solve(system, target, block=128):
    size = system.shape[0]
    count = size // block
    eye = jnp.eye(block, dtype=system.dtype)
    tiles = {
        (i, j): system[i * block : (i + 1) * block, j * block : (j + 1) * block]
        for i in range(count)
        for j in range(i + 1)
    }
    factors, inverses = {}, {}
    for j in range(count):
        diagonal = jnp.linalg.cholesky(tiles[j, j])
        inverse = jax.scipy.linalg.solve_triangular(diagonal, eye, lower=True)
        inverses[j] = inverse
        for i in range(j + 1, count):
            factors[i, j] = jnp.dot(tiles[i, j], inverse.T, precision=HIGH)
        for i in range(j + 1, count):
            for k in range(j + 1, i + 1):
                tiles[i, k] = tiles[i, k] - jnp.dot(factors[i, j], factors[k, j].T, precision=HIGH)
    parts = [target[j * block : (j + 1) * block] for j in range(count)]
    solved = []
    for j in range(count):
        rest = parts[j]
        for p in range(j):
            rest = rest - jnp.dot(factors[j, p], solved[p], precision=HIGH)
        solved.append(jnp.dot(inverses[j], rest, precision=HIGH))
    result = [None] * count
    for j in reversed(range(count)):
        rest = solved[j]
        for i in range(j + 1, count):
            rest = rest - jnp.dot(factors[i, j].T, result[i], precision=HIGH)
        result[j] = jnp.dot(inverses[j].T, rest, precision=HIGH)
    return jnp.concatenate(result, axis=0)


def _cholesky_solve_kernel(a_ref, b_ref, x_ref):
    a = a_ref[...]
    r = b_ref[...]
    n = a.shape[0]
    rows = jax.lax.broadcasted_iota(jnp.int32, r.shape, 0)
    cols = jax.lax.broadcasted_iota(jnp.int32, (1,) + a.shape[1:], 1)
    diags, columns = [], []
    for j in range(n):
        d = jnp.sqrt(a[j : j + 1, j : j + 1, :])
        column = jnp.where(rows >= j, a[:, j : j + 1, :] / d, 0.0)
        row = jnp.where(cols >= j, a[j : j + 1, :, :] / d, 0.0)
        a = a - column * row
        diags.append(d)
        columns.append(column)
    y = jnp.zeros_like(r)
    for j in range(n):
        yj = r[j : j + 1] / diags[j]
        r = r - columns[j] * yj
        y = jnp.where(rows == j, yj, y)
    x = jnp.zeros_like(r)
    for j in reversed(range(n)):
        s = jnp.sum(jnp.where(rows > j, columns[j] * x, 0.0), axis=0, keepdims=True)
        x = jnp.where(rows == j, (y[j : j + 1] - s) / diags[j], x)
    x_ref[...] = x


def cholesky_solve(systems, right_sides):
    batch, n, _ = systems.shape
    a = systems.transpose(1, 2, 0)
    b = right_sides.T[:, None, :]
    x = pl.pallas_call(
        _cholesky_solve_kernel,
        out_shape=jax.ShapeDtypeStruct((n, 1, batch), jnp.float32),
    )(a, b)
    return x[:, 0, :].T


def gather_a2a(value, name):
    n = lax.axis_size(name)
    copies = jnp.broadcast_to(value[None], (n,) + value.shape)
    return lax.all_to_all(copies, name, 0, 0, tiled=True)


def psum_tree(value):
    value = lax.psum(value, "c")
    for name in ("z", "x"):
        value = jnp.sum(gather_a2a(value, name), axis=0)
    return value


def shards(dosages, traits, folds):
    rows, width = dosages.shape
    traits_count = traits.shape[0]
    fold_ids = jnp.arange(FOLDS, dtype=jnp.int32)
    masks = (folds[None, :] == fold_ids[:, None]).astype(jnp.float32)
    mask_half = masks.astype(jnp.bfloat16)
    traits_wide = traits.astype(jnp.float32)
    augmented = jnp.concatenate(
        [dosages, jnp.ones((rows, 1), jnp.bfloat16), traits.T], axis=1
    )
    weighted = mask_half[:, :, None] * augmented[None]
    stats = jnp.einsum("ri,krj->kij", augmented, weighted, preferred_element_type=jnp.float32)
    stats = lax.psum(stats, SAMP)
    gram = stats[:, :width, :width]
    sums = stats[:, :width, width]
    counts = stats[:, width, width]
    cross = stats[:, width + 1 :, :width]
    trait_sums = stats[:, width + 1 :, width]
    total = jnp.sum(counts)
    mean = jnp.sum(sums, axis=0) / total
    gram_total = jnp.sum(gram, axis=0)
    variance = jnp.diagonal(gram_total) / total - mean * mean
    scale = lax.rsqrt(variance + EPS)
    sums_total = jnp.sum(sums, axis=0)
    cross_total = jnp.sum(cross, axis=0)
    trait_total = jnp.sum(trait_sums, axis=0)
    ratios = jnp.array(RATIOS, dtype=jnp.float32)
    identity = jnp.eye(width, dtype=jnp.float32)

    def train_system(fold):
        train_gram = gram_total - lax.dynamic_index_in_dim(gram, fold, 0, keepdims=False)
        train_sums = sums_total - lax.dynamic_index_in_dim(sums, fold, 0, keepdims=False)
        train_count = total - lax.dynamic_index_in_dim(counts, fold, 0, keepdims=False)
        train_cross = cross_total - lax.dynamic_index_in_dim(cross, fold, 0, keepdims=False)
        train_traits = trait_total - lax.dynamic_index_in_dim(trait_sums, fold, 0, keepdims=False)
        centered = (
            train_gram
            - mean[:, None] * train_sums[None, :]
            - train_sums[:, None] * mean[None, :]
            + train_count * mean[:, None] * mean[None, :]
        )
        system = scale[:, None] * centered * scale[None, :]
        target = scale[:, None] * (train_cross.T - mean[:, None] * train_traits[None, :])
        return (system, target)

    systems_count = FOLDS * SHRINK
    slots = lax.axis_size(("x", "z"))
    per_device = -(-systems_count // slots)
    first = lax.axis_index(("x", "z")) * per_device

    def solve_own(offset):
        which = jnp.minimum(first + offset, systems_count - 1)
        fold = which // SHRINK
        shrink = which - fold * SHRINK
        system, target = train_system(fold)
        penalty = jnp.sum(
            jnp.where(jnp.arange(SHRINK, dtype=jnp.int32) == shrink, ratios * width, 0.0)
        )
        beta = blocked_cholesky_solve(system + penalty * identity, target)
        return (scale[:, None] * beta).astype(jnp.bfloat16)

    owned = lax.map(solve_own, jnp.arange(per_device, dtype=jnp.int32))
    collected = gather_a2a(owned, "z")
    collected = gather_a2a(collected.reshape((-1,) + owned.shape[1:]), "x")
    collected = collected.reshape((-1,) + owned.shape[1:])
    coef = collected[:systems_count].reshape(FOLDS, SHRINK, width, traits_count)
    coef_flat = coef.transpose(2, 0, 1, 3).reshape(width, FOLDS * SHRINK * traits_count)
    shift = jnp.einsum("v,klvt->klt", mean, coef.astype(jnp.float32), precision=HIGH)
    raw = jnp.einsum("vc,rv->cr", coef_flat, dosages, preferred_element_type=jnp.float32)
    outcome = raw.reshape(FOLDS, SHRINK, traits_count, rows) - shift[..., None]
    level_pred = jnp.einsum("kltr,kr->ltr", outcome, masks, precision=HIGH)
    group = traits_count // lax.axis_size("blk")
    start = lax.axis_index("blk") * group
    own_traits = lax.dynamic_slice_in_dim(traits_wide, start, group, 0)
    own_sums = lax.dynamic_slice_in_dim(trait_sums, start, group, 1)
    arrived = lax.all_to_all(level_pred[None], "blk", split_axis=2, concat_axis=0, tiled=True)
    count_pred = arrived.shape[0] * arrived.shape[1]
    flat = arrived.reshape(count_pred, group, rows)
    raw_grams = jnp.einsum("ks,ats,bts->ktab", masks, flat, flat, precision=HIGH)
    raw_sums = jnp.einsum("ks,ats->kta", masks, flat, precision=HIGH)
    raw_cross = jnp.einsum("ks,ats,ts->kta", masks, flat, own_traits, precision=HIGH)
    packed = jnp.concatenate(
        [raw_grams.reshape(FOLDS * group, count_pred * count_pred),
         raw_sums.reshape(FOLDS * group, count_pred),
         raw_cross.reshape(FOLDS * group, count_pred)],
        axis=1,
    )
    packed = psum_tree(packed)
    raw_grams = packed[:, : count_pred * count_pred].reshape(FOLDS, group, count_pred, count_pred)
    raw_sums = packed[:, count_pred * count_pred : count_pred * (count_pred + 1)].reshape(
        FOLDS, group, count_pred
    )
    raw_cross = packed[:, count_pred * (count_pred + 1) :].reshape(FOLDS, group, count_pred)
    pred_sum = jnp.sum(raw_sums, axis=0)
    pred_sq = jnp.sum(jnp.diagonal(raw_grams, axis1=2, axis2=3), axis=0)
    pred_mean = pred_sum / total
    pred_var = pred_sq / total - pred_mean * pred_mean
    pred_scale = lax.rsqrt(pred_var + EPS)
    level0 = (flat - pred_mean.T[:, :, None]) * pred_scale.T[:, :, None]
    fold_mean = pred_mean[None]
    fold_sums = (raw_sums - counts[:, None, None] * fold_mean) * pred_scale[None]
    fold_grams = (
        raw_grams
        - fold_mean[..., :, None] * raw_sums[..., None, :]
        - raw_sums[..., :, None] * fold_mean[..., None, :]
        + counts[:, None, None, None] * fold_mean[..., :, None] * fold_mean[..., None, :]
    ) * (pred_scale[None, :, :, None] * pred_scale[None, :, None, :])
    fold_cross = (raw_cross - fold_mean * own_sums[:, :, None]) * pred_scale[None]
    level0 = level0.reshape(arrived.shape)
    train_grams = jnp.sum(fold_grams, axis=0)[None] - fold_grams
    train_cross = jnp.sum(fold_cross, axis=0)[None] - fold_cross
    shrunk = train_grams + total / 4.0 * jnp.eye(count_pred, dtype=jnp.float32)
    weights = cholesky_solve(
        shrunk.reshape(-1, count_pred, count_pred), train_cross.reshape(-1, count_pred)
    )
    weights = weights.reshape(FOLDS, group, count_pred)
    every_fold = jnp.einsum("ats,kta->kts", level0.reshape(flat.shape), weights, precision=HIGH)
    blended = jnp.einsum("kts,ks->ts", every_fold, masks, precision=HIGH)
    blend_sum = jnp.einsum("kta,kta->t", weights, fold_sums, precision=HIGH)
    blend_sq = jnp.einsum("kta,ktab,ktb->t", weights, fold_grams, weights, precision=HIGH)
    blend_mean = blend_sum / total
    blend_var = blend_sq / total - blend_mean * blend_mean
    blend = (blended - blend_mean[:, None]) * lax.rsqrt(blend_var + EPS)[:, None]
    return (level0, blend)


def view_of(mesh):
    devices = np.asarray(mesh.devices)
    samp, blk = devices.shape
    flat = list(devices.reshape(-1))
    xs = sorted({d.coords[0] for d in flat})
    zs = sorted({d.coords[2] for d in flat})
    cores = samp // (len(xs) * len(zs))
    view = devices.reshape(len(xs), len(zs), cores, blk)
    for (i, j, c, b), d in np.ndenumerate(view):
        assert d.coords[0] == xs[i] and d.coords[2] == zs[j]
    return Mesh(view, ("x", "z", "c", "blk"))


def solution(mesh):
    view = view_of(mesh)
    in_specs = (P(SAMP, "blk"), P(None, SAMP), P(SAMP))
    out_specs = (P(None, None, "blk", SAMP), P("blk", SAMP))
    return jax.shard_map(shards, mesh=view, in_specs=in_specs, out_specs=out_specs, check_vma=False)
```

```python
import jax
import jax.numpy as jnp
import numpy as np
from jax import lax
from jax.experimental import pallas as pl
from jax.sharding import Mesh
from jax.sharding import PartitionSpec as P

FOLDS = 5
SHRINK = 5


RATIOS = (99.0, 3.0, 1.0, 1.0 / 3.0, 1.0 / 99.0)
EPS = 1e-05
HIGH = lax.Precision.HIGHEST
SAMP = ("x", "z", "c")


def solve_batch(systems, right_sides):
    factors = jnp.linalg.cholesky(systems)

    def solve_single(factor, right_side):
        return jax.scipy.linalg.cho_solve((factor, True), right_side)

    return jax.vmap(solve_single)(factors, right_sides)


def blocked_cholesky_solve(system, target, block=128):
    size = system.shape[0]
    count = size // block
    eye = jnp.eye(block, dtype=system.dtype)
    tiles = {
        (i, j): system[i * block : (i + 1) * block, j * block : (j + 1) * block]
        for i in range(count)
        for j in range(i + 1)
    }
    factors, inverses = {}, {}
    for j in range(count):
        diagonal = jnp.linalg.cholesky(tiles[j, j])
        inverse = jax.scipy.linalg.solve_triangular(diagonal, eye, lower=True)
        inverses[j] = inverse
        for i in range(j + 1, count):
            factors[i, j] = jnp.dot(tiles[i, j], inverse.T, precision=HIGH)
        for i in range(j + 1, count):
            for k in range(j + 1, i + 1):
                tiles[i, k] = tiles[i, k] - jnp.dot(factors[i, j], factors[k, j].T, precision=HIGH)
    parts = [target[j * block : (j + 1) * block] for j in range(count)]
    solved = []
    for j in range(count):
        rest = parts[j]
        for p in range(j):
            rest = rest - jnp.dot(factors[j, p], solved[p], precision=HIGH)
        solved.append(jnp.dot(inverses[j], rest, precision=HIGH))
    result = [None] * count
    for j in reversed(range(count)):
        rest = solved[j]
        for i in range(j + 1, count):
            rest = rest - jnp.dot(factors[i, j].T, result[i], precision=HIGH)
        result[j] = jnp.dot(inverses[j].T, rest, precision=HIGH)
    return jnp.concatenate(result, axis=0)


def _cholesky_solve_kernel(a_ref, b_ref, x_ref):
    a = a_ref[...]
    r = b_ref[...]
    n = a.shape[0]
    rows = jax.lax.broadcasted_iota(jnp.int32, r.shape, 0)
    cols = jax.lax.broadcasted_iota(jnp.int32, (1,) + a.shape[1:], 1)
    diags, columns = [], []
    for j in range(n):
        d = jnp.sqrt(a[j : j + 1, j : j + 1, :])
        column = jnp.where(rows >= j, a[:, j : j + 1, :] / d, 0.0)
        row = jnp.where(cols >= j, a[j : j + 1, :, :] / d, 0.0)
        a = a - column * row
        diags.append(d)
        columns.append(column)
    y = jnp.zeros_like(r)
    for j in range(n):
        yj = r[j : j + 1] / diags[j]
        r = r - columns[j] * yj
        y = jnp.where(rows == j, yj, y)
    x = jnp.zeros_like(r)
    for j in reversed(range(n)):
        s = jnp.sum(jnp.where(rows > j, columns[j] * x, 0.0), axis=0, keepdims=True)
        x = jnp.where(rows == j, (y[j : j + 1] - s) / diags[j], x)
    x_ref[...] = x


def cholesky_solve(systems, right_sides):
    batch, n, _ = systems.shape
    a = systems.transpose(1, 2, 0)
    b = right_sides.T[:, None, :]
    x = pl.pallas_call(
        _cholesky_solve_kernel,
        out_shape=jax.ShapeDtypeStruct((n, 1, batch), jnp.float32),
    )(a, b)
    return x[:, 0, :].T


def gather_a2a(value, name):
    n = lax.axis_size(name)
    copies = jnp.broadcast_to(value[None], (n,) + value.shape)
    return lax.all_to_all(copies, name, 0, 0, tiled=True)


def psum_tree(value):
    value = lax.psum(value, "c")
    for name in ("z", "x"):
        value = jnp.sum(gather_a2a(value, name), axis=0)
    return value


def shards(dosages, traits, folds):
    rows, width = dosages.shape
    traits_count = traits.shape[0]
    fold_ids = jnp.arange(FOLDS, dtype=jnp.int32)
    masks = (folds[None, :] == fold_ids[:, None]).astype(jnp.float32)
    mask_half = masks.astype(jnp.bfloat16)
    traits_wide = traits.astype(jnp.float32)
    augmented = jnp.concatenate(
        [dosages, jnp.ones((rows, 1), jnp.bfloat16), traits.T], axis=1
    )
    weighted = mask_half[:, :, None] * augmented[None]
    stats = jnp.einsum("ri,krj->kij", augmented, weighted, preferred_element_type=jnp.float32)
    stats = lax.psum(stats, SAMP)
    gram = stats[:, :width, :width]
    sums = stats[:, :width, width]
    counts = stats[:, width, width]
    cross = stats[:, width + 1 :, :width]
    trait_sums = stats[:, width + 1 :, width]
    total = jnp.sum(counts)
    mean = jnp.sum(sums, axis=0) / total
    gram_total = jnp.sum(gram, axis=0)
    variance = jnp.sum(jnp.where(jnp.eye(width, dtype=jnp.bool_), gram_total, 0.0), axis=0) / total - mean * mean
    scale = lax.rsqrt(variance + EPS)
    sums_total = jnp.sum(sums, axis=0)
    cross_total = jnp.sum(cross, axis=0)
    trait_total = jnp.sum(trait_sums, axis=0)
    ratios = jnp.array(RATIOS, dtype=jnp.float32)
    identity = jnp.eye(width, dtype=jnp.float32)

    def train_system(fold):
        train_gram = gram_total - lax.dynamic_index_in_dim(gram, fold, 0, keepdims=False)
        train_sums = sums_total - lax.dynamic_index_in_dim(sums, fold, 0, keepdims=False)
        train_count = total - lax.dynamic_index_in_dim(counts, fold, 0, keepdims=False)
        train_cross = cross_total - lax.dynamic_index_in_dim(cross, fold, 0, keepdims=False)
        train_traits = trait_total - lax.dynamic_index_in_dim(trait_sums, fold, 0, keepdims=False)
        centered = (
            train_gram
            - mean[:, None] * train_sums[None, :]
            - train_sums[:, None] * mean[None, :]
            + train_count * mean[:, None] * mean[None, :]
        )
        system = scale[:, None] * centered * scale[None, :]
        target = scale[:, None] * (train_cross.T - mean[:, None] * train_traits[None, :])
        return (system, target)

    systems_count = FOLDS * SHRINK
    slots = lax.axis_size(("x", "z"))
    per_device = -(-systems_count // slots)
    first = lax.axis_index(("x", "z")) * per_device

    def solve_own(offset):
        which = jnp.minimum(first + offset, systems_count - 1)
        fold = which // SHRINK
        shrink = which - fold * SHRINK
        system, target = train_system(fold)
        penalty = jnp.sum(
            jnp.where(jnp.arange(SHRINK, dtype=jnp.int32) == shrink, ratios * width, 0.0)
        )
        beta = blocked_cholesky_solve(system + penalty * identity, target)
        return (scale[:, None] * beta).astype(jnp.bfloat16).T

    owned = lax.map(solve_own, jnp.arange(per_device, dtype=jnp.int32))
    collected = gather_a2a(owned, "z")
    collected = gather_a2a(collected.reshape((-1,) + owned.shape[1:]), "x")
    collected = collected.reshape((-1,) + owned.shape[1:])
    coef = collected[:systems_count].reshape(FOLDS, SHRINK, traits_count, width)
    coef_rows = coef.reshape(FOLDS * SHRINK * traits_count, width)
    shift = jnp.einsum("v,kltv->klt", mean, coef.astype(jnp.float32), precision=HIGH)
    raw = jnp.einsum("cv,rv->cr", coef_rows, dosages, preferred_element_type=jnp.float32)
    outcome = raw.reshape(FOLDS, SHRINK, traits_count, rows) - shift[..., None]
    level_pred = jnp.einsum("kltr,kr->ltr", outcome, masks, precision=HIGH)
    group = traits_count // lax.axis_size("blk")
    start = lax.axis_index("blk") * group
    own_traits = lax.dynamic_slice_in_dim(traits_wide, start, group, 0)
    own_sums = lax.dynamic_slice_in_dim(trait_sums, start, group, 1)
    arrived = lax.all_to_all(level_pred[None], "blk", split_axis=2, concat_axis=0, tiled=True)
    count_pred = arrived.shape[0] * arrived.shape[1]
    flat = arrived.reshape(count_pred, group, rows)
    raw_grams = jnp.einsum("ks,ats,bts->ktab", masks, flat, flat, precision=HIGH)
    raw_sums = jnp.einsum("ks,ats->kta", masks, flat, precision=HIGH)
    raw_cross = jnp.einsum("ks,ats,ts->kta", masks, flat, own_traits, precision=HIGH)
    packed = jnp.concatenate(
        [raw_grams.reshape(FOLDS * group, count_pred * count_pred),
         raw_sums.reshape(FOLDS * group, count_pred),
         raw_cross.reshape(FOLDS * group, count_pred)],
        axis=1,
    )
    packed = psum_tree(packed)
    raw_grams = packed[:, : count_pred * count_pred].reshape(FOLDS, group, count_pred, count_pred)
    raw_sums = packed[:, count_pred * count_pred : count_pred * (count_pred + 1)].reshape(
        FOLDS, group, count_pred
    )
    raw_cross = packed[:, count_pred * (count_pred + 1) :].reshape(FOLDS, group, count_pred)
    pred_sum = jnp.sum(raw_sums, axis=0)
    pred_sq = jnp.sum(jnp.diagonal(raw_grams, axis1=2, axis2=3), axis=0)
    pred_mean = pred_sum / total
    pred_var = pred_sq / total - pred_mean * pred_mean
    pred_scale = lax.rsqrt(pred_var + EPS)
    level0 = (flat - pred_mean.T[:, :, None]) * pred_scale.T[:, :, None]
    fold_mean = pred_mean[None]
    fold_sums = (raw_sums - counts[:, None, None] * fold_mean) * pred_scale[None]
    fold_grams = (
        raw_grams
        - fold_mean[..., :, None] * raw_sums[..., None, :]
        - raw_sums[..., :, None] * fold_mean[..., None, :]
        + counts[:, None, None, None] * fold_mean[..., :, None] * fold_mean[..., None, :]
    ) * (pred_scale[None, :, :, None] * pred_scale[None, :, None, :])
    fold_cross = (raw_cross - fold_mean * own_sums[:, :, None]) * pred_scale[None]
    level0 = level0.reshape(arrived.shape)
    train_grams = jnp.sum(fold_grams, axis=0)[None] - fold_grams
    train_cross = jnp.sum(fold_cross, axis=0)[None] - fold_cross
    shrunk = train_grams + total / 4.0 * jnp.eye(count_pred, dtype=jnp.float32)
    weights = cholesky_solve(
        shrunk.reshape(-1, count_pred, count_pred), train_cross.reshape(-1, count_pred)
    )
    weights = weights.reshape(FOLDS, group, count_pred)
    every_fold = jnp.einsum("ats,kta->kts", level0.reshape(flat.shape), weights, precision=HIGH)
    blended = jnp.einsum("kts,ks->ts", every_fold, masks, precision=HIGH)
    blend_sum = jnp.einsum("kta,kta->t", weights, fold_sums, precision=HIGH)
    blend_sq = jnp.einsum("kta,ktab,ktb->t", weights, fold_grams, weights, precision=HIGH)
    blend_mean = blend_sum / total
    blend_var = blend_sq / total - blend_mean * blend_mean
    blend = (blended - blend_mean[:, None]) * lax.rsqrt(blend_var + EPS)[:, None]
    return (level0, blend)


def view_of(mesh):
    devices = np.asarray(mesh.devices)
    samp, blk = devices.shape
    flat = list(devices.reshape(-1))
    xs = sorted({d.coords[0] for d in flat})
    zs = sorted({d.coords[2] for d in flat})
    cores = samp // (len(xs) * len(zs))
    view = devices.reshape(len(xs), len(zs), cores, blk)
    for (i, j, c, b), d in np.ndenumerate(view):
        assert d.coords[0] == xs[i] and d.coords[2] == zs[j]
    return Mesh(view, ("x", "z", "c", "blk"))


def solution(mesh):
    view = view_of(mesh)
    in_specs = (P(SAMP, "blk"), P(None, SAMP), P(SAMP))
    out_specs = (P(None, None, "blk", SAMP), P("blk", SAMP))
    return jax.shard_map(shards, mesh=view, in_specs=in_specs, out_specs=out_specs, check_vma=False)
```

```python
import jax
import jax.numpy as jnp
import numpy as np
from jax import lax
from jax.experimental import pallas as pl
from jax.sharding import Mesh
from jax.sharding import PartitionSpec as P

FOLDS = 5
SHRINK = 5


RATIOS = (99.0, 3.0, 1.0, 1.0 / 3.0, 1.0 / 99.0)
EPS = 1e-05
HIGH = lax.Precision.HIGHEST
SAMP = ("x", "z", "c")


def solve_batch(systems, right_sides):
    factors = jnp.linalg.cholesky(systems)

    def solve_single(factor, right_side):
        return jax.scipy.linalg.cho_solve((factor, True), right_side)

    return jax.vmap(solve_single)(factors, right_sides)


def blocked_cholesky_solve(system, target, block=128):
    size = system.shape[0]
    count = size // block
    eye = jnp.eye(block, dtype=system.dtype)
    tiles = {
        (i, j): system[i * block : (i + 1) * block, j * block : (j + 1) * block]
        for i in range(count)
        for j in range(i + 1)
    }
    factors, inverses = {}, {}
    for j in range(count):
        diagonal = jnp.linalg.cholesky(tiles[j, j])
        inverse = jax.scipy.linalg.solve_triangular(diagonal, eye, lower=True)
        inverses[j] = inverse
        for i in range(j + 1, count):
            factors[i, j] = jnp.dot(tiles[i, j], inverse.T, precision=HIGH)
        for i in range(j + 1, count):
            for k in range(j + 1, i + 1):
                tiles[i, k] = tiles[i, k] - jnp.dot(factors[i, j], factors[k, j].T, precision=HIGH)
    parts = [target[j * block : (j + 1) * block] for j in range(count)]
    solved = []
    for j in range(count):
        rest = parts[j]
        for p in range(j):
            rest = rest - jnp.dot(factors[j, p], solved[p], precision=HIGH)
        solved.append(jnp.dot(inverses[j], rest, precision=HIGH))
    result = [None] * count
    for j in reversed(range(count)):
        rest = solved[j]
        for i in range(j + 1, count):
            rest = rest - jnp.dot(factors[i, j].T, result[i], precision=HIGH)
        result[j] = jnp.dot(inverses[j].T, rest, precision=HIGH)
    return jnp.concatenate(result, axis=0)


def _cholesky_solve_kernel(a_ref, b_ref, x_ref):
    a = a_ref[...]
    r = b_ref[...]
    n = a.shape[0]
    rows = jax.lax.broadcasted_iota(jnp.int32, r.shape, 0)
    cols = jax.lax.broadcasted_iota(jnp.int32, (1,) + a.shape[1:], 1)
    diags, columns = [], []
    for j in range(n):
        d = jnp.sqrt(a[j : j + 1, j : j + 1, :])
        column = jnp.where(rows >= j, a[:, j : j + 1, :] / d, 0.0)
        row = jnp.where(cols >= j, a[j : j + 1, :, :] / d, 0.0)
        a = a - column * row
        diags.append(d)
        columns.append(column)
    y = jnp.zeros_like(r)
    for j in range(n):
        yj = r[j : j + 1] / diags[j]
        r = r - columns[j] * yj
        y = jnp.where(rows == j, yj, y)
    x = jnp.zeros_like(r)
    for j in reversed(range(n)):
        s = jnp.sum(jnp.where(rows > j, columns[j] * x, 0.0), axis=0, keepdims=True)
        x = jnp.where(rows == j, (y[j : j + 1] - s) / diags[j], x)
    x_ref[...] = x


def cholesky_solve(systems, right_sides):
    batch, n, _ = systems.shape
    a = systems.transpose(1, 2, 0)
    b = right_sides.T[:, None, :]
    x = pl.pallas_call(
        _cholesky_solve_kernel,
        out_shape=jax.ShapeDtypeStruct((n, 1, batch), jnp.float32),
    )(a, b)
    return x[:, 0, :].T


def gather_a2a(value, name):
    n = lax.axis_size(name)
    copies = jnp.broadcast_to(value[None], (n,) + value.shape)
    return lax.all_to_all(copies, name, 0, 0, tiled=True)


def psum_tree(value):
    value = lax.psum(value, "c")
    return jnp.sum(gather_a2a(value, ("x", "z")), axis=0)


def shards(dosages, traits, folds):
    rows, width = dosages.shape
    traits_count = traits.shape[0]
    fold_ids = jnp.arange(FOLDS, dtype=jnp.int32)
    masks = (folds[None, :] == fold_ids[:, None]).astype(jnp.float32)
    mask_half = masks.astype(jnp.bfloat16)
    traits_wide = traits.astype(jnp.float32)
    augmented = jnp.concatenate(
        [dosages, jnp.ones((rows, 1), jnp.bfloat16), traits.T], axis=1
    )
    weighted = mask_half[:, :, None] * augmented[None]
    stats = jnp.einsum("ri,krj->kij", augmented, weighted, preferred_element_type=jnp.float32)
    stats = lax.psum(stats, SAMP)
    gram = stats[:, :width, :width]
    sums = stats[:, :width, width]
    counts = stats[:, width, width]
    cross = stats[:, width + 1 :, :width]
    trait_sums = stats[:, width + 1 :, width]
    total = jnp.sum(counts)
    mean = jnp.sum(sums, axis=0) / total
    gram_total = jnp.sum(gram, axis=0)
    variance = jnp.sum(jnp.where(jnp.eye(width, dtype=jnp.bool_), gram_total, 0.0), axis=0) / total - mean * mean
    scale = lax.rsqrt(variance + EPS)
    sums_total = jnp.sum(sums, axis=0)
    cross_total = jnp.sum(cross, axis=0)
    trait_total = jnp.sum(trait_sums, axis=0)
    ratios = jnp.array(RATIOS, dtype=jnp.float32)
    identity = jnp.eye(width, dtype=jnp.float32)

    def train_system(fold):
        train_gram = gram_total - lax.dynamic_index_in_dim(gram, fold, 0, keepdims=False)
        train_sums = sums_total - lax.dynamic_index_in_dim(sums, fold, 0, keepdims=False)
        train_count = total - lax.dynamic_index_in_dim(counts, fold, 0, keepdims=False)
        train_cross = cross_total - lax.dynamic_index_in_dim(cross, fold, 0, keepdims=False)
        train_traits = trait_total - lax.dynamic_index_in_dim(trait_sums, fold, 0, keepdims=False)
        centered = (
            train_gram
            - mean[:, None] * train_sums[None, :]
            - train_sums[:, None] * mean[None, :]
            + train_count * mean[:, None] * mean[None, :]
        )
        system = scale[:, None] * centered * scale[None, :]
        target = scale[:, None] * (train_cross.T - mean[:, None] * train_traits[None, :])
        return (system, target)

    systems_count = FOLDS * SHRINK
    slots = lax.axis_size(("x", "z"))
    per_device = -(-systems_count // slots)
    first = lax.axis_index(("x", "z")) * per_device

    def solve_own(offset):
        which = jnp.minimum(first + offset, systems_count - 1)
        fold = which // SHRINK
        shrink = which - fold * SHRINK
        system, target = train_system(fold)
        penalty = jnp.sum(
            jnp.where(jnp.arange(SHRINK, dtype=jnp.int32) == shrink, ratios * width, 0.0)
        )
        beta = blocked_cholesky_solve(system + penalty * identity, target)
        return (scale[:, None] * beta).astype(jnp.bfloat16).T

    owned = lax.map(solve_own, jnp.arange(per_device, dtype=jnp.int32))
    collected = gather_a2a(owned, ("x", "z")).reshape((-1,) + owned.shape[1:])
    coef = collected[:systems_count].reshape(FOLDS, SHRINK, traits_count, width)
    coef_rows = coef.reshape(FOLDS * SHRINK * traits_count, width)
    shift = jnp.einsum("v,kltv->klt", mean, coef.astype(jnp.float32), precision=HIGH)
    raw = jnp.einsum("cv,rv->cr", coef_rows, dosages, preferred_element_type=jnp.float32)
    outcome = raw.reshape(FOLDS, SHRINK, traits_count, rows) - shift[..., None]
    level_pred = jnp.einsum("kltr,kr->ltr", outcome, masks, precision=HIGH)
    group = traits_count // lax.axis_size("blk")
    start = lax.axis_index("blk") * group
    own_traits = lax.dynamic_slice_in_dim(traits_wide, start, group, 0)
    own_sums = lax.dynamic_slice_in_dim(trait_sums, start, group, 1)
    arrived = lax.all_to_all(level_pred[None], "blk", split_axis=2, concat_axis=0, tiled=True)
    count_pred = arrived.shape[0] * arrived.shape[1]
    flat = arrived.reshape(count_pred, group, rows)
    raw_grams = jnp.einsum("ks,ats,bts->ktab", masks, flat, flat, precision=HIGH)
    raw_sums = jnp.einsum("ks,ats->kta", masks, flat, precision=HIGH)
    raw_cross = jnp.einsum("ks,ats,ts->kta", masks, flat, own_traits, precision=HIGH)
    packed = jnp.concatenate(
        [raw_grams.reshape(FOLDS * group, count_pred * count_pred),
         raw_sums.reshape(FOLDS * group, count_pred),
         raw_cross.reshape(FOLDS * group, count_pred)],
        axis=1,
    )
    packed = psum_tree(packed)
    raw_grams = packed[:, : count_pred * count_pred].reshape(FOLDS, group, count_pred, count_pred)
    raw_sums = packed[:, count_pred * count_pred : count_pred * (count_pred + 1)].reshape(
        FOLDS, group, count_pred
    )
    raw_cross = packed[:, count_pred * (count_pred + 1) :].reshape(FOLDS, group, count_pred)
    pred_sum = jnp.sum(raw_sums, axis=0)
    pred_sq = jnp.sum(jnp.diagonal(raw_grams, axis1=2, axis2=3), axis=0)
    pred_mean = pred_sum / total
    pred_var = pred_sq / total - pred_mean * pred_mean
    pred_scale = lax.rsqrt(pred_var + EPS)
    level0 = (flat - pred_mean.T[:, :, None]) * pred_scale.T[:, :, None]
    fold_mean = pred_mean[None]
    fold_sums = (raw_sums - counts[:, None, None] * fold_mean) * pred_scale[None]
    fold_grams = (
        raw_grams
        - fold_mean[..., :, None] * raw_sums[..., None, :]
        - raw_sums[..., :, None] * fold_mean[..., None, :]
        + counts[:, None, None, None] * fold_mean[..., :, None] * fold_mean[..., None, :]
    ) * (pred_scale[None, :, :, None] * pred_scale[None, :, None, :])
    fold_cross = (raw_cross - fold_mean * own_sums[:, :, None]) * pred_scale[None]
    level0 = level0.reshape(arrived.shape)
    train_grams = jnp.sum(fold_grams, axis=0)[None] - fold_grams
    train_cross = jnp.sum(fold_cross, axis=0)[None] - fold_cross
    shrunk = train_grams + total / 4.0 * jnp.eye(count_pred, dtype=jnp.float32)
    weights = cholesky_solve(
        shrunk.reshape(-1, count_pred, count_pred), train_cross.reshape(-1, count_pred)
    )
    weights = weights.reshape(FOLDS, group, count_pred)
    every_fold = jnp.einsum("ats,kta->kts", level0.reshape(flat.shape), weights, precision=HIGH)
    blended = jnp.einsum("kts,ks->ts", every_fold, masks, precision=HIGH)
    blend_sum = jnp.einsum("kta,kta->t", weights, fold_sums, precision=HIGH)
    blend_sq = jnp.einsum("kta,ktab,ktb->t", weights, fold_grams, weights, precision=HIGH)
    blend_mean = blend_sum / total
    blend_var = blend_sq / total - blend_mean * blend_mean
    blend = (blended - blend_mean[:, None]) * lax.rsqrt(blend_var + EPS)[:, None]
    return (level0, blend)


def view_of(mesh):
    devices = np.asarray(mesh.devices)
    samp, blk = devices.shape
    flat = list(devices.reshape(-1))
    xs = sorted({d.coords[0] for d in flat})
    zs = sorted({d.coords[2] for d in flat})
    cores = samp // (len(xs) * len(zs))
    view = devices.reshape(len(xs), len(zs), cores, blk)
    for (i, j, c, b), d in np.ndenumerate(view):
        assert d.coords[0] == xs[i] and d.coords[2] == zs[j]
    return Mesh(view, ("x", "z", "c", "blk"))


def solution(mesh):
    view = view_of(mesh)
    in_specs = (P(SAMP, "blk"), P(None, SAMP), P(SAMP))
    out_specs = (P(None, None, "blk", SAMP), P("blk", SAMP))
    return jax.shard_map(shards, mesh=view, in_specs=in_specs, out_specs=out_specs, check_vma=False)
```
